32 devices in a mesh: ctx: 8 (over y, x, core), dp: 4 (over z).
Axes of the slice: x: 2, y: 2, z: 4, core: 2. Of those that a mesh axis runs over, the one named last changes fastest.
Arguments:
- tokens: bfloat16 [4, 1024, 4096], P('dp', 'ctx'), may hold values from -64 to 64
- query_weight: bfloat16 [4096, 4096], P('dp', 'ctx'), may hold values from -0.09375 to 0.09375
- keyval_matrix: bfloat16 [4096, 1024], P('dp', 'ctx'), may hold values from -0.09375 to 0.09375
- grad_out: bfloat16 [4, 1024, 4096], P('dp', 'ctx'), may hold values from -6 to 6
- blocks: int32 [4, 8, 8], replicated, may hold values from 0 to 7, as said below
- counts: int32 [4, 8], replicated, may hold values from 4 to 8, as said below
Outputs:
- attended: bfloat16 [4, 1024, 4096], P('dp', 'ctx')
- grad_query_weight: float32 [4096, 4096], P('dp', 'ctx')
- grad_keyval_weight: float32 [4096, 1024], P('dp', 'ctx')
The draws below stay inside these ranges and needn't reach their ends.
Inputs may be any that keep to these rules, and one draw needn't show every extreme that they name: For key head g and query block i, the first counts[g, i] entries of blocks[g, i] are distinct; they are the blocks i - 1, i, i + 1, 0 and 7 that exist, then random others. Entries from counts[g, i] on are block numbers that are not attended. counts[g, i] is the number of distinct blocks among i - 1, i, i + 1, 0 and 7 that exist, plus 1 to 3.
All inputs are finite; a program needn't handle non-finite values.
Results may differ from the reference program's by a relative error of at most 0.004.
The reference program's roundings to bfloat16 on the way count: a program that leaves them out, or rounds other values in their place, can miss the bound.
Values may be sent and summed in bfloat16 or wider, within the bound.
No kernel may reach another device: no remote copies, remote signals or barrier semaphores. Data moves between devices by JAX's collectives and lax.ppermute only.
A program may use at most 128 MiB of HBM per device.

```python
import jax
import jax.numpy as jnp
from jax import lax

MODEL_WIDTH = 4096
QUERY_HEADS = 32
KEY_HEADS = 4
HEAD_WIDTH = 128
BLOCK_POSITIONS = 128
RANDOM_BLOCKS = 3
KB = 8
SEQUENCE_LENGTH = 1024
SEQUENCE_BLOCKS = 8
SEQS = 4


def block_lists(key):
    first_key_block = jax.random.fold_in(key, 71)
    row_ids = jnp.arange(SEQUENCE_BLOCKS, dtype=jnp.int32)[:, None]
    column_index = jnp.arange(SEQUENCE_BLOCKS, dtype=jnp.int32)[None, :]
    base_offset = (jnp.abs(row_ids - column_index) <= 1) | (column_index == 0) | (column_index == SEQUENCE_BLOCKS - 1)
    key_rows = jax.random.split(first_key_block, KEY_HEADS * SEQUENCE_BLOCKS)
    sorting_index = jax.vmap(lambda key_block: jax.random.permutation(key_block, SEQUENCE_BLOCKS))(key_rows).reshape(KEY_HEADS, SEQUENCE_BLOCKS, SEQUENCE_BLOCKS).astype(jnp.int32)
    sorted_blocks = jnp.where(base_offset[None], jnp.broadcast_to(column_index[None], (KEY_HEADS, SEQUENCE_BLOCKS, SEQUENCE_BLOCKS)), SEQUENCE_BLOCKS + sorting_index)
    picked = jnp.argsort(sorted_blocks, axis=-1, stable=True)[:, :, :KB].astype(jnp.int32)
    base_count = jnp.sum(base_offset.astype(jnp.int32), axis=-1)
    additional = jax.random.randint(jax.random.fold_in(key, 72), (KEY_HEADS, SEQUENCE_BLOCKS), 1, RANDOM_BLOCKS + 1).astype(jnp.int32)
    additional = additional.at[0, 0].set(1)
    additional = additional.at[0, SEQUENCE_BLOCKS // 2].set(RANDOM_BLOCKS)
    live = (base_count[None, :] + additional).astype(jnp.int32)
    return (picked, live)


def draw_blocks(key, part):
    return block_lists(key)[0]


def draw_counts(key, part):
    return block_lists(key)[1]


def draw_tokens(key, part):
    first = jax.random.fold_in(key, 0)
    values = jnp.clip(jax.random.normal(first, (SEQS, SEQUENCE_LENGTH, MODEL_WIDTH), jnp.float32), -6.0, 6.0)
    return values.astype(jnp.bfloat16)


def level_of(stream_key, extent, shards, least, largest):
    gain, own = 1.0, jax.random.fold_in(stream_key, 6)
    for position, parts in shards:
        steps = jnp.exp(jax.random.uniform(jax.random.fold_in(own, position), (parts,), jnp.float32, least / len(shards), largest / len(shards)))
        gain = gain * jnp.repeat(steps, extent[position] // parts).reshape([-1 if axis == position else 1 for axis in range(len(extent))])
    return gain


def centred(rng, dims, scale, limit, shards=(), held_as=jnp.bfloat16):
    loudness = level_of(rng, dims, shards, -0.22, 0.18) if shards else 1.0
    drawn = jax.random.normal(rng, dims, jnp.float32) * scale * loudness
    return jnp.minimum(jnp.maximum(drawn, -limit), limit).astype(held_as)


def setup_inputs(seed: int = 0) -> dict:
    splits = jax.random.split(jax.random.key(seed), 7)
    return {
        "tokens": draw_tokens(jax.random.fold_in(splits[6], 71), 0),
        "query_weight": centred(splits[1], (MODEL_WIDTH, QUERY_HEADS * HEAD_WIDTH), MODEL_WIDTH ** -0.5, 0.09375, ((0, 4), (1, 8))),
        "keyval_matrix": centred(splits[2], (MODEL_WIDTH, 2 * KEY_HEADS * HEAD_WIDTH), MODEL_WIDTH ** -0.5, 0.09375, ((0, 4), (1, 8))),
        "grad_out": centred(splits[3], (SEQS, SEQUENCE_LENGTH, QUERY_HEADS * HEAD_WIDTH), 1.0, 6.0, ((0, 4), (1, 8))),
        "blocks": draw_blocks(jax.random.fold_in(splits[6], 71), 0),
        "counts": draw_counts(jax.random.fold_in(splits[6], 71), 0),
    }


def attend(q, key_rows, vals, dout, blk, cnt):
    nb, kslots = blk.shape
    scale = q.shape[-1] ** -0.5
    kb = key_rows[blk].astype(jnp.float32)
    vb = vals[blk].astype(jnp.float32)
    valid = lax.broadcasted_iota(jnp.int32, (nb, kslots), 1) < cnt[:, None]
    qf = q.astype(jnp.float32)
    df = dout.astype(jnp.float32)
    scores = jnp.einsum("nqhd,nkcd->nhqkc", qf, kb) * scale
    scores = jnp.where(valid[:, None, None, :, None], scores, -jnp.inf)
    peak = jnp.max(scores, axis=(3, 4), keepdims=True)
    expo = jnp.exp(scores - peak)
    probs = expo / jnp.sum(expo, axis=(3, 4), keepdims=True)
    probs_b = probs.astype(jnp.bfloat16)
    pf = probs_b.astype(jnp.float32)
    out = jnp.einsum("nhqkc,nkcd->nqhd", pf, vb).astype(jnp.bfloat16)
    delta = jnp.transpose(jnp.sum(df * out.astype(jnp.float32), axis=3), (0, 2, 1))
    dprob = jnp.einsum("nqhd,nkcd->nhqkc", df, vb)
    dscore = (probs * (dprob - delta[:, :, :, None, None]) * scale).astype(jnp.bfloat16)
    sf = dscore.astype(jnp.float32)
    dq = jnp.einsum("nhqkc,nkcd->nqhd", sf, kb).astype(jnp.bfloat16)
    dkb = jnp.einsum("nhqkc,nqhd->nkcd", sf, qf)
    dvb = jnp.einsum("nhqkc,nqhd->nkcd", pf, df)
    onehot = ((blk[None, :, :] == lax.broadcasted_iota(jnp.int32, (nb, 1, 1), 0)) & valid[None]).astype(jnp.float32)
    dk = jnp.einsum("bnk,nkcd->bcd", onehot, dkb, precision=lax.Precision.HIGHEST)
    dv = jnp.einsum("bnk,nkcd->bcd", onehot, dvb, precision=lax.Precision.HIGHEST)
    return out, dq, dk, dv


def reference(tokens, query_weight, keyval_matrix, grad_out, blocks, counts):
    heads_per_group = QUERY_HEADS // KEY_HEADS

    def one_sequence(carry, inputs):
        rows, output_gradients = inputs
        query_rows = jnp.dot(rows, query_weight, preferred_element_type=jnp.float32).astype(jnp.bfloat16)
        keyval_rows = jnp.dot(rows, keyval_matrix, preferred_element_type=jnp.float32).astype(jnp.bfloat16)
        query_rows = jnp.transpose(query_rows.reshape(SEQUENCE_BLOCKS, BLOCK_POSITIONS, KEY_HEADS, heads_per_group, HEAD_WIDTH), (2, 0, 1, 3, 4))
        keyval_rows = jnp.transpose(keyval_rows.reshape(SEQUENCE_BLOCKS, BLOCK_POSITIONS, KEY_HEADS, 2, HEAD_WIDTH), (2, 3, 0, 1, 4))
        group_output_gradients = jnp.transpose(output_gradients.reshape(SEQUENCE_BLOCKS, BLOCK_POSITIONS, KEY_HEADS, heads_per_group, HEAD_WIDTH), (2, 0, 1, 3, 4))

        def one_group(args):
            qg, kvg, dg, bg, cg = args
            return attend(qg, kvg[0], kvg[1], dg, bg, cg)

        out, dq, dk, dv = lax.map(one_group, (query_rows, keyval_rows, group_output_gradients, blocks, counts))
        out = jnp.transpose(out, (1, 2, 0, 3, 4)).reshape(SEQUENCE_LENGTH, QUERY_HEADS * HEAD_WIDTH)
        dq = jnp.transpose(dq, (1, 2, 0, 3, 4)).reshape(SEQUENCE_LENGTH, QUERY_HEADS * HEAD_WIDTH)
        keyval_gradient = jnp.stack([dk, dv], axis=1)
        keyval_gradient = jnp.transpose(keyval_gradient, (2, 3, 0, 1, 4)).reshape(SEQUENCE_LENGTH, 2 * KEY_HEADS * HEAD_WIDTH).astype(jnp.bfloat16)
        grad_q = lax.dot_general(rows, dq, (((0,), (0,)), ((), ())), preferred_element_type=jnp.float32)
        grad_kv = lax.dot_general(rows, keyval_gradient, (((0,), (0,)), ((), ())), preferred_element_type=jnp.float32)
        return (carry[0] + grad_q, carry[1] + grad_kv), out

    start_position = (jnp.zeros((MODEL_WIDTH, QUERY_HEADS * HEAD_WIDTH), jnp.float32), jnp.zeros((MODEL_WIDTH, 2 * KEY_HEADS * HEAD_WIDTH), jnp.float32))
    grads, attended = lax.scan(one_sequence, start_position, (tokens, grad_out))
    return attended, grads[0], grads[1]
```

```python
import jax
import jax.numpy as jnp
from jax import lax
from jax.sharding import PartitionSpec as P


def partner(block, axis, distance):
    count = lax.axis_size(axis)
    route = []
    for low in range(count):
        high = low | 1 << distance
        if high != low and high < count:
            route += [(low, high), (high, low)]
    return lax.ppermute(block, axis, route)


def attend_part(query_rows, key_rows, vals, dout, valid, scale):
    scores = (
        jnp.einsum("nqhd,nkcd->nhqkc", query_rows, key_rows, preferred_element_type=jnp.float32)
        * scale
    )
    scores = jnp.where(valid[:, None, None, :, None], scores, -jnp.inf)
    peak = jnp.max(scores, axis=(3, 4), keepdims=True)
    expo = jnp.exp(scores - peak)
    probs = expo / jnp.sum(expo, axis=(3, 4), keepdims=True)
    probs_b = probs.astype(jnp.bfloat16)
    out = jnp.einsum("nhqkc,nkcd->nqhd", probs_b, vals, preferred_element_type=jnp.float32).astype(
        jnp.bfloat16
    )
    delta = jnp.transpose(
        jnp.sum(dout.astype(jnp.float32) * out.astype(jnp.float32), axis=3), (0, 2, 1)
    )
    dprob = jnp.einsum("nqhd,nkcd->nhqkc", dout, vals, preferred_element_type=jnp.float32)
    dscore = (probs * (dprob - delta[:, :, :, None, None]) * scale).astype(jnp.bfloat16)
    dquery = jnp.einsum(
        "nhqkc,nkcd->nqhd", dscore, key_rows, preferred_element_type=jnp.float32
    ).astype(jnp.bfloat16)
    dkeys = jnp.einsum("nhqkc,nqhd->nkcd", dscore, query_rows, preferred_element_type=jnp.float32)
    dvals = jnp.einsum("nhqkc,nqhd->nkcd", probs_b, dout, preferred_element_type=jnp.float32)
    return (out, dquery, dkeys, dvals)


def attention(q_heads, keyval_rows, dout_heads, blk, cnt):
    length = q_heads.shape[0]
    head_size = keyval_rows.shape[1] // 2
    heads = q_heads.shape[1] // head_size
    nblocks, kslots = blk.shape
    block = length // nblocks
    scale = head_size ** (-0.5)
    step = 4
    groups = nblocks // step
    key_rows = keyval_rows[:, :head_size].reshape(nblocks, block, head_size)
    vals = keyval_rows[:, head_size:].reshape(nblocks, block, head_size)
    valid = lax.broadcasted_iota(jnp.int32, (nblocks, kslots), 1) < cnt[:, None]
    query_rows = q_heads.reshape(groups, step, block, heads, head_size)
    dout = dout_heads.reshape(groups, step, block, heads, head_size)

    def one_step(args):
        q_part, d_part, b_part, v_part = args
        return attend_part(q_part, key_rows[b_part], vals[b_part], d_part, v_part, scale)

    out, dquery, dkeys, dvals = lax.map(
        one_step,
        (query_rows, dout, blk.reshape(groups, step, kslots), valid.reshape(groups, step, kslots)),
    )
    dkeys = dkeys.reshape(nblocks, kslots, block, head_size)
    dvals = dvals.reshape(nblocks, kslots, block, head_size)
    onehot = (
        (blk[None, :, :] == lax.broadcasted_iota(jnp.int32, (nblocks, 1, 1), 0)) & valid[None]
    ).astype(jnp.float32)
    key_grad = jnp.einsum("bnk,nkcd->bcd", onehot, dkeys, precision=lax.Precision.HIGHEST)
    val_grad = jnp.einsum("bnk,nkcd->bcd", onehot, dvals, precision=lax.Precision.HIGHEST)
    keyval_grad = jnp.concatenate(
        [key_grad.reshape(length, head_size), val_grad.reshape(length, head_size)], axis=1
    )
    return (
        out.reshape(length, heads * head_size),
        dquery.reshape(length, heads * head_size),
        keyval_grad,
    )


def shards(tokens, query_weight, keyval_matrix, grad_out, blocks, counts):
    local_rows = tokens[0]
    group_size = lax.axis_size("ctx") // blocks.shape[0]
    group_bits = group_size.bit_length() - 1
    device = lax.axis_index("ctx")
    query_cols = query_weight.shape[1]
    weights_full = lax.all_gather(
        jnp.concatenate([query_weight, keyval_matrix], axis=1), "dp", axis=0, tiled=True
    )
    query_full = weights_full[:, :query_cols]
    keyval_part = weights_full[:, query_cols:]
    all_rows = lax.all_gather(local_rows, "ctx", axis=0, tiled=True)
    keyval_cols = keyval_part
    for bit in range(group_bits):
        other = partner(keyval_cols, "ctx", bit)
        upper = device >> bit & 1 == 1
        keyval_cols = jnp.where(
            upper,
            jnp.concatenate([other, keyval_cols], axis=1),
            jnp.concatenate([keyval_cols, other], axis=1),
        )
    projected = jnp.dot(
        all_rows,
        jnp.concatenate([query_full, keyval_cols], axis=1),
        preferred_element_type=jnp.float32,
    ).astype(jnp.bfloat16)
    q_heads = projected[:, :query_cols]
    keyval_rows = projected[:, query_cols:]
    dout_heads = lax.all_to_all(grad_out[0], "ctx", split_axis=1, concat_axis=0, tiled=True)
    group_index = device // group_size
    blk = lax.dynamic_index_in_dim(blocks, group_index, 0, keepdims=False)
    cnt = lax.dynamic_index_in_dim(counts, group_index, 0, keepdims=False)
    out_heads, dquery, keyval_grad = attention(q_heads, keyval_rows, dout_heads, blk, cnt)
    attended = lax.all_to_all(out_heads, "ctx", split_axis=0, concat_axis=1, tiled=True)
    summed = keyval_grad
    for bit in range(group_bits):
        summed = summed + partner(summed, "ctx", bit)
    width = summed.shape[1] // group_size
    own_grad = lax.dynamic_slice_in_dim(summed, device % group_size * width, width, 1)
    own_grad = own_grad.astype(jnp.bfloat16)
    contract = (((0,), (0,)), ((), ()))
    grad_query = lax.dot_general(all_rows, dquery, contract, preferred_element_type=jnp.float32)
    grad_keyval = lax.dot_general(all_rows, own_grad, contract, preferred_element_type=jnp.float32)
    grads = lax.psum_scatter(
        jnp.concatenate([grad_query, grad_keyval], axis=1), "dp", scatter_dimension=0, tiled=True
    )
    grad_query = grads[:, :query_cols]
    grad_keyval = grads[:, query_cols:]
    return (attended[None], grad_query, grad_keyval)


def solution(mesh):
    in_specs = (
        P("dp", "ctx", None),
        P("dp", "ctx"),
        P("dp", "ctx"),
        P("dp", "ctx", None),
        P(),
        P(),
    )
    out_specs = (P("dp", "ctx", None), P("dp", "ctx"), P("dp", "ctx"))
    return jax.shard_map(shards, mesh=mesh, in_specs=in_specs, out_specs=out_specs, check_vma=False)
```

```python
import jax
import jax.numpy as jnp
from jax import lax
from jax.sharding import PartitionSpec as P


def partner(block, axis, distance):
    count = lax.axis_size(axis)
    route = []
    for low in range(count):
        high = low | 1 << distance
        if high != low and high < count:
            route += [(low, high), (high, low)]
    return lax.ppermute(block, axis, route)


def attend_part(query_rows, key_rows, vals, dout, valid, scale):
    scores = (
        jnp.einsum("nqhd,nkcd->nhqkc", query_rows, key_rows, preferred_element_type=jnp.float32)
        * scale
    )
    scores = jnp.where(valid[:, None, None, :, None], scores, -jnp.inf)
    peak = jnp.max(scores, axis=(3, 4), keepdims=True)
    expo = jnp.exp(scores - peak)
    probs = expo / jnp.sum(expo, axis=(3, 4), keepdims=True)
    probs_b = probs.astype(jnp.bfloat16)
    out = jnp.einsum("nhqkc,nkcd->nqhd", probs_b, vals, preferred_element_type=jnp.float32).astype(
        jnp.bfloat16
    )
    delta = jnp.transpose(
        jnp.sum(dout.astype(jnp.float32) * out.astype(jnp.float32), axis=3), (0, 2, 1)
    )
    dprob = jnp.einsum("nqhd,nkcd->nhqkc", dout, vals, preferred_element_type=jnp.float32)
    dscore = (probs * (dprob - delta[:, :, :, None, None]) * scale).astype(jnp.bfloat16)
    dquery = jnp.einsum(
        "nhqkc,nkcd->nqhd", dscore, key_rows, preferred_element_type=jnp.float32
    ).astype(jnp.bfloat16)
    dkeys = jnp.einsum("nhqkc,nqhd->nkcd", dscore, query_rows, preferred_element_type=jnp.float32)
    dvals = jnp.einsum("nhqkc,nqhd->nkcd", probs_b, dout, preferred_element_type=jnp.float32)
    return (out, dquery, dkeys, dvals)


def attention(q_heads, keyval_rows, dout_heads, blk, cnt):
    length = q_heads.shape[0]
    head_size = keyval_rows.shape[1] // 2
    heads = q_heads.shape[1] // head_size
    nblocks, kslots = blk.shape
    block = length // nblocks
    scale = head_size ** (-0.5)
    step = 4
    groups = nblocks // step
    key_rows = keyval_rows[:, :head_size].reshape(nblocks, block, head_size)
    vals = keyval_rows[:, head_size:].reshape(nblocks, block, head_size)
    valid = lax.broadcasted_iota(jnp.int32, (nblocks, kslots), 1) < cnt[:, None]
    query_rows = q_heads.reshape(groups, step, block, heads, head_size)
    dout = dout_heads.reshape(groups, step, block, heads, head_size)

    def one_step(args):
        q_part, d_part, b_part, v_part = args
        return attend_part(q_part, key_rows[b_part], vals[b_part], d_part, v_part, scale)

    out, dquery, dkeys, dvals = lax.map(
        one_step,
        (query_rows, dout, blk.reshape(groups, step, kslots), valid.reshape(groups, step, kslots)),
    )
    dkeys = dkeys.reshape(nblocks, kslots, block, head_size)
    dvals = dvals.reshape(nblocks, kslots, block, head_size)
    onehot = (
        (blk[None, :, :] == lax.broadcasted_iota(jnp.int32, (nblocks, 1, 1), 0)) & valid[None]
    ).astype(jnp.float32)
    key_grad = jnp.einsum("bnk,nkcd->bcd", onehot, dkeys, precision=lax.Precision.HIGHEST)
    val_grad = jnp.einsum("bnk,nkcd->bcd", onehot, dvals, precision=lax.Precision.HIGHEST)
    keyval_grad = jnp.concatenate(
        [key_grad.reshape(length, head_size), val_grad.reshape(length, head_size)], axis=1
    )
    return (
        out.reshape(length, heads * head_size),
        dquery.reshape(length, heads * head_size),
        keyval_grad,
    )


def shards(tokens, query_weight, keyval_matrix, grad_out, blocks, counts):
    local_rows = tokens[0]
    dp_size = lax.axis_size("dp")
    row_block = local_rows.shape[1] // dp_size
    row_slices = lax.all_to_all(
        local_rows.reshape(local_rows.shape[0], dp_size, row_block).transpose(1, 0, 2),
        "dp", split_axis=0, concat_axis=0, tiled=True,
    )
    group_size = lax.axis_size("ctx") // blocks.shape[0]
    group_bits = group_size.bit_length() - 1
    device = lax.axis_index("ctx")
    query_cols = query_weight.shape[1]
    weights_full = lax.all_gather(
        jnp.concatenate([query_weight, keyval_matrix], axis=1), "dp", axis=0, tiled=True
    )
    query_full = weights_full[:, :query_cols]
    keyval_part = weights_full[:, query_cols:]
    all_rows = lax.all_gather(local_rows, "ctx", axis=0, tiled=True)
    keyval_cols = keyval_part
    for bit in range(group_bits):
        other = partner(keyval_cols, "ctx", bit)
        upper = device >> bit & 1 == 1
        keyval_cols = jnp.where(
            upper,
            jnp.concatenate([other, keyval_cols], axis=1),
            jnp.concatenate([keyval_cols, other], axis=1),
        )
    projected = jnp.dot(
        all_rows,
        jnp.concatenate([query_full, keyval_cols], axis=1),
        preferred_element_type=jnp.float32,
    ).astype(jnp.bfloat16)
    q_heads = projected[:, :query_cols]
    keyval_rows = projected[:, query_cols:]
    dout_heads = lax.all_to_all(grad_out[0], "ctx", split_axis=1, concat_axis=0, tiled=True)
    group_index = device // group_size
    blk = lax.dynamic_index_in_dim(blocks, group_index, 0, keepdims=False)
    cnt = lax.dynamic_index_in_dim(counts, group_index, 0, keepdims=False)
    out_heads, dquery, keyval_grad = attention(q_heads, keyval_rows, dout_heads, blk, cnt)
    attended = lax.all_to_all(out_heads, "ctx", split_axis=0, concat_axis=1, tiled=True)
    summed = keyval_grad
    for bit in range(group_bits):
        summed = summed + partner(summed, "ctx", bit)
    width = summed.shape[1] // group_size
    own_grad = lax.dynamic_slice_in_dim(summed, device % group_size * width, width, 1)
    own_grad = own_grad.astype(jnp.bfloat16)
    cotangents = lax.all_gather(
        jnp.concatenate([dquery, own_grad], axis=1), "dp", axis=0, tiled=False
    )
    row_tokens = lax.all_gather(row_slices, "ctx", axis=1, tiled=True)
    grads = jnp.einsum(
        "spr,spk->rk", row_tokens, cotangents, preferred_element_type=jnp.float32
    )
    grad_query = grads[:, :query_cols]
    grad_keyval = grads[:, query_cols:]
    return (attended[None], grad_query, grad_keyval)


def solution(mesh):
    in_specs = (
        P("dp", "ctx", None),
        P("dp", "ctx"),
        P("dp", "ctx"),
        P("dp", "ctx", None),
        P(),
        P(),
    )
    out_specs = (P("dp", "ctx", None), P("dp", "ctx"), P("dp", "ctx"))
    return jax.shard_map(shards, mesh=mesh, in_specs=in_specs, out_specs=out_specs, check_vma=False)
```

```python
import jax
import jax.numpy as jnp
from jax import lax
from jax.sharding import PartitionSpec as P


def partner(block, axis, distance):
    count = lax.axis_size(axis)
    route = []
    for low in range(count):
        high = low | 1 << distance
        if high != low and high < count:
            route += [(low, high), (high, low)]
    return lax.ppermute(block, axis, route)


def attend_part(query_rows, key_rows, vals, dout, valid, scale):
    scores = (
        jnp.einsum("nqhd,nkcd->nhqkc", query_rows, key_rows, preferred_element_type=jnp.float32)
        * scale
    )
    scores = jnp.where(valid[:, None, None, :, None], scores, -jnp.inf)
    peak = jnp.max(scores, axis=(3, 4), keepdims=True)
    expo = jnp.exp(scores - peak)
    probs = expo / jnp.sum(expo, axis=(3, 4), keepdims=True)
    probs_b = probs.astype(jnp.bfloat16)
    out = jnp.einsum("nhqkc,nkcd->nqhd", probs_b, vals, preferred_element_type=jnp.float32).astype(
        jnp.bfloat16
    )
    delta = jnp.transpose(
        jnp.sum(dout.astype(jnp.float32) * out.astype(jnp.float32), axis=3), (0, 2, 1)
    )
    dprob = jnp.einsum("nqhd,nkcd->nhqkc", dout, vals, preferred_element_type=jnp.float32)
    dscore = (probs * (dprob - delta[:, :, :, None, None]) * scale).astype(jnp.bfloat16)
    dquery = jnp.einsum(
        "nhqkc,nkcd->nqhd", dscore, key_rows, preferred_element_type=jnp.float32
    ).astype(jnp.bfloat16)
    dkeys = jnp.einsum("nhqkc,nqhd->nkcd", dscore, query_rows, preferred_element_type=jnp.float32)
    dvals = jnp.einsum("nhqkc,nqhd->nkcd", probs_b, dout, preferred_element_type=jnp.float32)
    return (out, dquery, dkeys, dvals)


def attention(q_heads, keyval_rows, dout_heads, blk, cnt):
    length = q_heads.shape[0]
    head_size = keyval_rows.shape[1] // 2
    heads = q_heads.shape[1] // head_size
    nblocks, kslots = blk.shape
    block = length // nblocks
    scale = head_size ** (-0.5)
    step = 4
    groups = nblocks // step
    key_rows = keyval_rows[:, :head_size].reshape(nblocks, block, head_size)
    vals = keyval_rows[:, head_size:].reshape(nblocks, block, head_size)
    valid = lax.broadcasted_iota(jnp.int32, (nblocks, kslots), 1) < cnt[:, None]
    query_rows = q_heads.reshape(groups, step, block, heads, head_size)
    dout = dout_heads.reshape(groups, step, block, heads, head_size)

    def one_step(args):
        q_part, d_part, b_part, v_part = args
        return attend_part(q_part, key_rows[b_part], vals[b_part], d_part, v_part, scale)

    out, dquery, dkeys, dvals = lax.map(
        one_step,
        (query_rows, dout, blk.reshape(groups, step, kslots), valid.reshape(groups, step, kslots)),
    )
    dkeys = dkeys.reshape(nblocks, kslots, block, head_size)
    dvals = dvals.reshape(nblocks, kslots, block, head_size)
    onehot = (
        (blk[None, :, :] == lax.broadcasted_iota(jnp.int32, (nblocks, 1, 1), 0)) & valid[None]
    ).astype(jnp.float32)
    key_grad = jnp.einsum("bnk,nkcd->bcd", onehot, dkeys, precision=lax.Precision.HIGHEST)
    val_grad = jnp.einsum("bnk,nkcd->bcd", onehot, dvals, precision=lax.Precision.HIGHEST)
    keyval_grad = jnp.concatenate(
        [key_grad.reshape(length, head_size), val_grad.reshape(length, head_size)], axis=1
    )
    return (
        out.reshape(length, heads * head_size),
        dquery.reshape(length, heads * head_size),
        keyval_grad,
    )


def gather_blocks(block, axis):
    count = lax.axis_size(axis)
    bits = count.bit_length() - 1
    order = list(range(1, bits)) + [0] if bits > 0 else []
    held = block[None]
    for bit in order:
        held = jnp.concatenate([held, partner(held, axis, bit)], axis=0)
    me = lax.axis_index(axis)
    wanted = lax.broadcasted_iota(jnp.int32, (count,), 0) ^ me
    slot = jnp.zeros((count,), jnp.int32)
    for place, bit in enumerate(order):
        slot = slot | ((wanted >> bit) & 1) << place
    held = jnp.take(held, slot, axis=0, mode="clip")
    return held.reshape((count * block.shape[0],) + block.shape[1:])


def shards(tokens, query_weight, keyval_matrix, grad_out, blocks, counts):
    local_rows = tokens[0]
    dp_size = lax.axis_size("dp")
    row_block = local_rows.shape[1] // dp_size
    group_size = lax.axis_size("ctx") // blocks.shape[0]
    group_bits = group_size.bit_length() - 1
    device = lax.axis_index("ctx")
    query_cols = query_weight.shape[1]
    head_size = keyval_matrix.shape[1] * group_size // 2
    heads = query_cols // head_size
    chunks = 2 if heads % 2 == 0 else 1
    chunk_cols = query_cols // chunks
    row_slices = lax.all_to_all(
        local_rows.reshape(local_rows.shape[0], dp_size, row_block).transpose(1, 0, 2),
        "dp", split_axis=0, concat_axis=0, tiled=True,
    )
    first_weights = lax.all_gather(
        jnp.concatenate([query_weight[:, :chunk_cols], keyval_matrix], axis=1),
        "dp", axis=0, tiled=True,
    )
    later_weights = [
        lax.all_gather(query_weight[:, k * chunk_cols:(k + 1) * chunk_cols], "dp", axis=0, tiled=True)
        for k in range(1, chunks)
    ]
    all_rows = gather_blocks(local_rows, "ctx")
    keyval_cols = first_weights[:, chunk_cols:]
    for bit in range(group_bits):
        other = partner(keyval_cols, "ctx", bit)
        upper = device >> bit & 1 == 1
        keyval_cols = jnp.where(
            upper,
            jnp.concatenate([other, keyval_cols], axis=1),
            jnp.concatenate([keyval_cols, other], axis=1),
        )
    projected = jnp.dot(
        all_rows,
        jnp.concatenate([first_weights[:, :chunk_cols], keyval_cols], axis=1),
        preferred_element_type=jnp.float32,
    ).astype(jnp.bfloat16)
    keyval_rows = projected[:, chunk_cols:]
    q_parts = [projected[:, :chunk_cols]] + [
        jnp.dot(all_rows, w, preferred_element_type=jnp.float32).astype(jnp.bfloat16)
        for w in later_weights
    ]
    dout_heads = lax.all_to_all(grad_out[0], "ctx", split_axis=1, concat_axis=0, tiled=True)
    group_index = device // group_size
    blk = lax.dynamic_index_in_dim(blocks, group_index, 0, keepdims=False)
    cnt = lax.dynamic_index_in_dim(counts, group_index, 0, keepdims=False)
    row_tokens = gather_blocks(row_slices.transpose(1, 0, 2), "ctx")
    outs, keyval_grad, grads = [], None, []
    contract = (((0, 1), (0, 1)), ((), ()))
    for k in range(chunks):
        out_part, dquery, kv_part = attention(
            q_parts[k], keyval_rows, dout_heads[:, k * chunk_cols:(k + 1) * chunk_cols], blk, cnt
        )
        outs.append(out_part)
        keyval_grad = kv_part if keyval_grad is None else keyval_grad + kv_part
        if k == chunks - 1:
            summed = keyval_grad
            for bit in range(group_bits):
                summed = summed + partner(summed, "ctx", bit)
            width = summed.shape[1] // group_size
            own_grad = lax.dynamic_slice_in_dim(summed, device % group_size * width, width, 1)
            dquery = jnp.concatenate([dquery, own_grad.astype(jnp.bfloat16)], axis=1)
        cotangents = lax.all_gather(dquery, "dp", axis=1, tiled=False)
        grads.append(
            lax.dot_general(row_tokens, cotangents, contract, preferred_element_type=jnp.float32)
        )
    attended = lax.all_to_all(
        jnp.concatenate(outs, axis=1), "ctx", split_axis=0, concat_axis=1, tiled=True
    )
    grads = jnp.concatenate(grads, axis=1)
    return (attended[None], grads[:, :query_cols], grads[:, query_cols:])


def solution(mesh):
    in_specs = (
        P("dp", "ctx", None),
        P("dp", "ctx"),
        P("dp", "ctx"),
        P("dp", "ctx", None),
        P(),
        P(),
    )
    out_specs = (P("dp", "ctx", None), P("dp", "ctx"), P("dp", "ctx"))
    return jax.shard_map(shards, mesh=mesh, in_specs=in_specs, out_specs=out_specs, check_vma=False)
```

```python
import jax
import jax.numpy as jnp
from jax import lax
from jax.sharding import PartitionSpec as P


def partner(block, axis, distance):
    count = lax.axis_size(axis)
    route = []
    for low in range(count):
        high = low | 1 << distance
        if high != low and high < count:
            route += [(low, high), (high, low)]
    return lax.ppermute(block, axis, route)


def attend_part(query_rows, key_rows, vals, dout, valid, scale):
    scores = (
        jnp.einsum("nqhd,nkcd->nhqkc", query_rows, key_rows, preferred_element_type=jnp.float32)
        * scale
    )
    scores = jnp.where(valid[:, None, None, :, None], scores, -jnp.inf)
    peak = jnp.max(scores, axis=(3, 4), keepdims=True)
    expo = jnp.exp(scores - peak)
    probs = expo / jnp.sum(expo, axis=(3, 4), keepdims=True)
    probs_b = probs.astype(jnp.bfloat16)
    out = jnp.einsum("nhqkc,nkcd->nqhd", probs_b, vals, preferred_element_type=jnp.float32).astype(
        jnp.bfloat16
    )
    delta = jnp.transpose(
        jnp.sum(dout.astype(jnp.float32) * out.astype(jnp.float32), axis=3), (0, 2, 1)
    )
    dprob = jnp.einsum("nqhd,nkcd->nhqkc", dout, vals, preferred_element_type=jnp.float32)
    dscore = (probs * (dprob - delta[:, :, :, None, None]) * scale).astype(jnp.bfloat16)
    dquery = jnp.einsum(
        "nhqkc,nkcd->nqhd", dscore, key_rows, preferred_element_type=jnp.float32
    ).astype(jnp.bfloat16)
    dkeys = jnp.einsum("nhqkc,nqhd->nkcd", dscore, query_rows, preferred_element_type=jnp.float32)
    dvals = jnp.einsum("nhqkc,nqhd->nkcd", probs_b, dout, preferred_element_type=jnp.float32)
    return (out, dquery, dkeys, dvals)


def attention(q_heads, keyval_rows, dout_heads, blk, cnt):
    length = q_heads.shape[0]
    head_size = keyval_rows.shape[1] // 2
    heads = q_heads.shape[1] // head_size
    nblocks, kslots = blk.shape
    block = length // nblocks
    scale = head_size ** (-0.5)
    step = 4
    groups = nblocks // step
    key_rows = keyval_rows[:, :head_size].reshape(nblocks, block, head_size)
    vals = keyval_rows[:, head_size:].reshape(nblocks, block, head_size)
    valid = lax.broadcasted_iota(jnp.int32, (nblocks, kslots), 1) < cnt[:, None]
    query_rows = q_heads.reshape(groups, step, block, heads, head_size)
    dout = dout_heads.reshape(groups, step, block, heads, head_size)

    def one_step(args):
        q_part, d_part, b_part, v_part = args
        return attend_part(q_part, key_rows[b_part], vals[b_part], d_part, v_part, scale)

    out, dquery, dkeys, dvals = lax.map(
        one_step,
        (query_rows, dout, blk.reshape(groups, step, kslots), valid.reshape(groups, step, kslots)),
    )
    return (
        out.reshape(length, heads * head_size),
        dquery.reshape(length, heads * head_size),
        (dkeys, dvals),
    )


def scatter_slots(dkeys, dvals, blk, cnt):
    nblocks, kslots = blk.shape
    block, head_size = dkeys.shape[-2:]
    length = nblocks * block
    valid = lax.broadcasted_iota(jnp.int32, (nblocks, kslots), 1) < cnt[:, None]
    dkeys = dkeys.reshape(nblocks, kslots, block, head_size)
    dvals = dvals.reshape(nblocks, kslots, block, head_size)
    onehot = (
        (blk[None, :, :] == lax.broadcasted_iota(jnp.int32, (nblocks, 1, 1), 0)) & valid[None]
    ).astype(jnp.float32)
    key_grad = jnp.einsum("bnk,nkcd->bcd", onehot, dkeys, precision=lax.Precision.HIGHEST)
    val_grad = jnp.einsum("bnk,nkcd->bcd", onehot, dvals, precision=lax.Precision.HIGHEST)
    keyval_grad = jnp.concatenate(
        [key_grad.reshape(length, head_size), val_grad.reshape(length, head_size)], axis=1
    )
    return keyval_grad


def gather_blocks(block, axis, dim):
    count = lax.axis_size(axis)
    bits = count.bit_length() - 1
    order = list(range(1, bits)) + [0] if bits > 0 else []
    held = jnp.expand_dims(block, dim)
    for bit in order:
        held = jnp.concatenate([held, partner(held, axis, bit)], axis=dim)
    spread = jnp.zeros((count,), jnp.int32)
    slots = lax.broadcasted_iota(jnp.int32, (count,), 0)
    for place, bit in enumerate(order):
        spread = spread | ((slots >> place) & 1) << bit
    return held, spread ^ lax.axis_index(axis)


def shards(tokens, query_weight, keyval_matrix, grad_out, blocks, counts):
    local_rows = tokens[0]
    dp_size = lax.axis_size("dp")
    row_block = local_rows.shape[1] // dp_size
    group_size = lax.axis_size("ctx") // blocks.shape[0]
    group_bits = group_size.bit_length() - 1
    device = lax.axis_index("ctx")
    query_cols = query_weight.shape[1]
    head_size = keyval_matrix.shape[1] * group_size // 2
    heads = query_cols // head_size
    chunks = 2 if heads % 2 == 0 else 1
    chunk_cols = query_cols // chunks
    row_slices = lax.all_to_all(
        local_rows.reshape(local_rows.shape[0], dp_size, row_block).transpose(1, 0, 2),
        "dp", split_axis=0, concat_axis=0, tiled=True,
    )
    first_weights = lax.all_gather(
        jnp.concatenate([query_weight[:, :chunk_cols], keyval_matrix], axis=1),
        "dp", axis=0, tiled=True,
    )
    later_weights = [
        lax.all_gather(query_weight[:, k * chunk_cols:(k + 1) * chunk_cols], "dp", axis=0, tiled=True)
        for k in range(1, chunks)
    ]
    all_rows = lax.all_gather(local_rows, "ctx", axis=0, tiled=True)
    keyval_cols = first_weights[:, chunk_cols:]
    for bit in range(group_bits):
        other = partner(keyval_cols, "ctx", bit)
        upper = device >> bit & 1 == 1
        keyval_cols = jnp.where(
            upper,
            jnp.concatenate([other, keyval_cols], axis=1),
            jnp.concatenate([keyval_cols, other], axis=1),
        )
    projected = jnp.dot(
        all_rows,
        jnp.concatenate([first_weights[:, :chunk_cols], keyval_cols], axis=1),
        preferred_element_type=jnp.float32,
    ).astype(jnp.bfloat16)
    keyval_rows = projected[:, chunk_cols:]
    q_parts = [projected[:, :chunk_cols]] + [
        jnp.dot(all_rows, w, preferred_element_type=jnp.float32).astype(jnp.bfloat16)
        for w in later_weights
    ]
    dout_heads = lax.all_to_all(grad_out[0], "ctx", split_axis=1, concat_axis=0, tiled=True)
    group_index = device // group_size
    blk = lax.dynamic_index_in_dim(blocks, group_index, 0, keepdims=False)
    cnt = lax.dynamic_index_in_dim(counts, group_index, 0, keepdims=False)
    row_tokens, source = gather_blocks(row_slices, "ctx", 1)
    nblocks = blk.shape[0]

    def slot_order(rows):
        rows = rows.reshape((nblocks, rows.shape[0] // nblocks) + rows.shape[1:])
        return jnp.take(rows, source, axis=0, mode="clip").reshape((-1,) + rows.shape[2:])

    outs, partials, grads = [], None, []
    contract = (((0, 1, 2), (0, 1, 2)), ((), ()))
    for k in range(chunks):
        out_part, dquery, part = attention(
            q_parts[k], keyval_rows, dout_heads[:, k * chunk_cols:(k + 1) * chunk_cols], blk, cnt
        )
        outs.append(out_part)
        partials = part if partials is None else (partials[0] + part[0], partials[1] + part[1])
        if k == chunks - 1:
            summed = scatter_slots(partials[0], partials[1], blk, cnt)
            for bit in range(group_bits):
                summed = summed + partner(summed, "ctx", bit)
            width = summed.shape[1] // group_size
            own_grad = lax.dynamic_slice_in_dim(summed, device % group_size * width, width, 1)
            dquery = jnp.concatenate([dquery, own_grad.astype(jnp.bfloat16)], axis=1)
        cotangents = lax.all_gather(slot_order(dquery), "dp", axis=0, tiled=False)
        cotangents = cotangents.reshape(
            (dp_size, nblocks, cotangents.shape[1] // nblocks, cotangents.shape[2])
        )
        grads.append(
            lax.dot_general(row_tokens, cotangents, contract, preferred_element_type=jnp.float32)
        )
    attended = lax.all_to_all(
        jnp.concatenate(outs, axis=1), "ctx", split_axis=0, concat_axis=1, tiled=True
    )
    grads = jnp.concatenate(grads, axis=1)
    return (attended[None], grads[:, :query_cols], grads[:, query_cols:])


def solution(mesh):
    in_specs = (
        P("dp", "ctx", None),
        P("dp", "ctx"),
        P("dp", "ctx"),
        P("dp", "ctx", None),
        P(),
        P(),
    )
    out_specs = (P("dp", "ctx", None), P("dp", "ctx"), P("dp", "ctx"))
    return jax.shard_map(shards, mesh=mesh, in_specs=in_specs, out_specs=out_specs, check_vma=False)
```

```python
import jax
import jax.numpy as jnp
from jax import lax
from jax.sharding import PartitionSpec as P


def partner(block, axis, distance):
    count = lax.axis_size(axis)
    route = []
    for low in range(count):
        high = low | 1 << distance
        if high != low and high < count:
            route += [(low, high), (high, low)]
    return lax.ppermute(block, axis, route)


def attend_part(query_rows, key_rows, vals, dout, valid, scale):
    scores = (
        jnp.einsum("nqhd,nkcd->nhqkc", query_rows, key_rows, preferred_element_type=jnp.float32)
        * scale
    )
    scores = jnp.where(valid[:, None, None, :, None], scores, -jnp.inf)
    peak = jnp.max(scores, axis=(3, 4), keepdims=True)
    expo = jnp.exp(scores - peak)
    probs = expo / jnp.sum(expo, axis=(3, 4), keepdims=True)
    probs_b = probs.astype(jnp.bfloat16)
    out = jnp.einsum("nhqkc,nkcd->nqhd", probs_b, vals, preferred_element_type=jnp.float32).astype(
        jnp.bfloat16
    )
    delta = jnp.transpose(
        jnp.sum(dout.astype(jnp.float32) * out.astype(jnp.float32), axis=3), (0, 2, 1)
    )
    dprob = jnp.einsum("nqhd,nkcd->nhqkc", dout, vals, preferred_element_type=jnp.float32)
    dscore = (probs * (dprob - delta[:, :, :, None, None]) * scale).astype(jnp.bfloat16)
    dquery = jnp.einsum(
        "nhqkc,nkcd->nqhd", dscore, key_rows, preferred_element_type=jnp.float32
    ).astype(jnp.bfloat16)
    dkeys = jnp.einsum("nhqkc,nqhd->nkcd", dscore, query_rows, preferred_element_type=jnp.float32)
    dvals = jnp.einsum("nhqkc,nqhd->nkcd", probs_b, dout, preferred_element_type=jnp.float32)
    return (out, dquery, dkeys, dvals)


def attention(q_heads, keyval_rows, dout_heads, blk, cnt):
    length = q_heads.shape[0]
    head_size = keyval_rows.shape[1] // 2
    heads = q_heads.shape[1] // head_size
    nblocks, kslots = blk.shape
    block = length // nblocks
    scale = head_size ** (-0.5)
    step = 4
    groups = nblocks // step
    key_rows = keyval_rows[:, :head_size].reshape(nblocks, block, head_size)
    vals = keyval_rows[:, head_size:].reshape(nblocks, block, head_size)
    valid = lax.broadcasted_iota(jnp.int32, (nblocks, kslots), 1) < cnt[:, None]
    query_rows = q_heads.reshape(groups, step, block, heads, head_size)
    dout = dout_heads.reshape(groups, step, block, heads, head_size)

    def one_step(args):
        q_part, d_part, b_part, v_part = args
        return attend_part(q_part, key_rows[b_part], vals[b_part], d_part, v_part, scale)

    out, dquery, dkeys, dvals = lax.map(
        one_step,
        (query_rows, dout, blk.reshape(groups, step, kslots), valid.reshape(groups, step, kslots)),
    )
    dkeys = dkeys.reshape(nblocks, kslots, block, head_size)
    dvals = dvals.reshape(nblocks, kslots, block, head_size)
    onehot = (
        (blk[None, :, :] == lax.broadcasted_iota(jnp.int32, (nblocks, 1, 1), 0)) & valid[None]
    ).astype(jnp.float32)
    key_grad = jnp.einsum("bnk,nkcd->bcd", onehot, dkeys, precision=lax.Precision.HIGHEST)
    val_grad = jnp.einsum("bnk,nkcd->bcd", onehot, dvals, precision=lax.Precision.HIGHEST)
    keyval_grad = jnp.concatenate(
        [key_grad.reshape(length, head_size), val_grad.reshape(length, head_size)], axis=1
    )
    return (
        out.reshape(length, heads * head_size),
        dquery.reshape(length, heads * head_size),
        keyval_grad,
    )


def exchange_gather(block, axis, order):
    count = lax.axis_size(axis)
    held = block[None]
    for bit in order:
        held = jnp.concatenate([held, partner(held, axis, bit)], axis=0)
    wanted = lax.broadcasted_iota(jnp.int32, (count,), 0) ^ lax.axis_index(axis)
    slot = jnp.zeros((count,), jnp.int32)
    for place, bit in enumerate(order):
        slot = slot | ((wanted >> bit) & 1) << place
    return jnp.take(held, slot, axis=0, mode="clip")


def gather_rows(rows, axis):
    bits = lax.axis_size(axis).bit_length() - 1
    upper = list(range(1, bits))
    half = rows.shape[0] // 2
    first = exchange_gather(rows[:half], axis, upper + [0] if bits else [])
    second = exchange_gather(rows[half:], axis, upper[::-1] + [0] if bits else [])
    return jnp.concatenate([first, second], axis=1).reshape((-1,) + rows.shape[1:])


def shards(tokens, query_weight, keyval_matrix, grad_out, blocks, counts):
    local_rows = tokens[0]
    dp_size = lax.axis_size("dp")
    row_block = local_rows.shape[1] // dp_size
    row_slices = lax.all_to_all(
        local_rows.reshape(local_rows.shape[0], dp_size, row_block).transpose(1, 0, 2),
        "dp", split_axis=0, concat_axis=0, tiled=True,
    )
    group_size = lax.axis_size("ctx") // blocks.shape[0]
    group_bits = group_size.bit_length() - 1
    device = lax.axis_index("ctx")
    query_cols = query_weight.shape[1]
    weights_full = lax.all_gather(
        jnp.concatenate([query_weight, keyval_matrix], axis=1), "dp", axis=0, tiled=True
    )
    query_full = weights_full[:, :query_cols]
    keyval_part = weights_full[:, query_cols:]
    all_rows = gather_rows(local_rows, "ctx")
    keyval_cols = keyval_part
    for bit in range(group_bits):
        other = partner(keyval_cols, "ctx", bit)
        upper = device >> bit & 1 == 1
        keyval_cols = jnp.where(
            upper,
            jnp.concatenate([other, keyval_cols], axis=1),
            jnp.concatenate([keyval_cols, other], axis=1),
        )
    projected = jnp.dot(
        all_rows,
        jnp.concatenate([query_full, keyval_cols], axis=1),
        preferred_element_type=jnp.float32,
    ).astype(jnp.bfloat16)
    q_heads = projected[:, :query_cols]
    keyval_rows = projected[:, query_cols:]
    dout_heads = lax.all_to_all(grad_out[0], "ctx", split_axis=1, concat_axis=0, tiled=True)
    group_index = device // group_size
    blk = lax.dynamic_index_in_dim(blocks, group_index, 0, keepdims=False)
    cnt = lax.dynamic_index_in_dim(counts, group_index, 0, keepdims=False)
    out_heads, dquery, keyval_grad = attention(q_heads, keyval_rows, dout_heads, blk, cnt)
    attended = lax.all_to_all(out_heads, "ctx", split_axis=0, concat_axis=1, tiled=True)
    summed = keyval_grad
    for bit in range(group_bits):
        summed = summed + partner(summed, "ctx", bit)
    width = summed.shape[1] // group_size
    own_grad = lax.dynamic_slice_in_dim(summed, device % group_size * width, width, 1)
    own_grad = own_grad.astype(jnp.bfloat16)
    cotangents = lax.all_gather(
        jnp.concatenate([dquery, own_grad], axis=1), "dp", axis=0, tiled=False
    )
    row_tokens = lax.all_gather(row_slices, "ctx", axis=1, tiled=True)
    grads = jnp.einsum(
        "spr,spk->rk", row_tokens, cotangents, preferred_element_type=jnp.float32
    )
    grad_query = grads[:, :query_cols]
    grad_keyval = grads[:, query_cols:]
    return (attended[None], grad_query, grad_keyval)


def solution(mesh):
    in_specs = (
        P("dp", "ctx", None),
        P("dp", "ctx"),
        P("dp", "ctx"),
        P("dp", "ctx", None),
        P(),
        P(),
    )
    out_specs = (P("dp", "ctx", None), P("dp", "ctx"), P("dp", "ctx"))
    return jax.shard_map(shards, mesh=mesh, in_specs=in_specs, out_specs=out_specs, check_vma=False)
```

```python
import jax
import jax.numpy as jnp
from jax import lax
from jax.sharding import PartitionSpec as P


def partner(block, axis, distance):
    count = lax.axis_size(axis)
    route = []
    for low in range(count):
        high = low | 1 << distance
        if high != low and high < count:
            route += [(low, high), (high, low)]
    return lax.ppermute(block, axis, route)


def attend_part(query_rows, key_rows, vals, dout, valid, scale):
    scores = (
        jnp.einsum("nqhd,nkcd->nhqkc", query_rows, key_rows, preferred_element_type=jnp.float32)
        * scale
    )
    scores = jnp.where(valid[:, None, None, :, None], scores, -jnp.inf)
    peak = jnp.max(scores, axis=(3, 4), keepdims=True)
    expo = jnp.exp(scores - peak)
    probs = expo / jnp.sum(expo, axis=(3, 4), keepdims=True)
    probs_b = probs.astype(jnp.bfloat16)
    out = jnp.einsum("nhqkc,nkcd->nqhd", probs_b, vals, preferred_element_type=jnp.float32).astype(
        jnp.bfloat16
    )
    delta = jnp.transpose(
        jnp.sum(dout.astype(jnp.float32) * out.astype(jnp.float32), axis=3), (0, 2, 1)
    )
    dprob = jnp.einsum("nqhd,nkcd->nhqkc", dout, vals, preferred_element_type=jnp.float32)
    dscore = (probs * (dprob - delta[:, :, :, None, None]) * scale).astype(jnp.bfloat16)
    dquery = jnp.einsum(
        "nhqkc,nkcd->nqhd", dscore, key_rows, preferred_element_type=jnp.float32
    ).astype(jnp.bfloat16)
    dkeys = jnp.einsum("nhqkc,nqhd->nkcd", dscore, query_rows, preferred_element_type=jnp.float32)
    dvals = jnp.einsum("nhqkc,nqhd->nkcd", probs_b, dout, preferred_element_type=jnp.float32)
    return (out, dquery, dkeys, dvals)


def attention(q_heads, keyval_rows, dout_heads, blk, cnt):
    length = q_heads.shape[0]
    head_size = keyval_rows.shape[1] // 2
    heads = q_heads.shape[1] // head_size
    nblocks, kslots = blk.shape
    block = length // nblocks
    scale = head_size ** (-0.5)
    step = 4
    groups = nblocks // step
    key_rows = keyval_rows[:, :head_size].reshape(nblocks, block, head_size)
    vals = keyval_rows[:, head_size:].reshape(nblocks, block, head_size)
    valid = lax.broadcasted_iota(jnp.int32, (nblocks, kslots), 1) < cnt[:, None]
    query_rows = q_heads.reshape(groups, step, block, heads, head_size)
    dout = dout_heads.reshape(groups, step, block, heads, head_size)

    def one_step(args):
        q_part, d_part, b_part, v_part = args
        return attend_part(q_part, key_rows[b_part], vals[b_part], d_part, v_part, scale)

    out, dquery, dkeys, dvals = lax.map(
        one_step,
        (query_rows, dout, blk.reshape(groups, step, kslots), valid.reshape(groups, step, kslots)),
    )
    dkeys = dkeys.reshape(nblocks, kslots, block, head_size)
    dvals = dvals.reshape(nblocks, kslots, block, head_size)
    onehot = (
        (blk[None, :, :] == lax.broadcasted_iota(jnp.int32, (nblocks, 1, 1), 0)) & valid[None]
    ).astype(jnp.float32)
    key_grad = jnp.einsum("bnk,nkcd->bcd", onehot, dkeys, precision=lax.Precision.HIGHEST)
    val_grad = jnp.einsum("bnk,nkcd->bcd", onehot, dvals, precision=lax.Precision.HIGHEST)
    keyval_grad = jnp.concatenate(
        [key_grad.reshape(length, head_size), val_grad.reshape(length, head_size)], axis=1
    )
    return (
        out.reshape(length, heads * head_size),
        dquery.reshape(length, heads * head_size),
        keyval_grad,
    )


def exchange_gather(block, axis, order):
    count = lax.axis_size(axis)
    held = block[None]
    for bit in order:
        held = jnp.concatenate([held, partner(held, axis, bit)], axis=0)
    wanted = lax.broadcasted_iota(jnp.int32, (count,), 0) ^ lax.axis_index(axis)
    slot = jnp.zeros((count,), jnp.int32)
    for place, bit in enumerate(order):
        slot = slot | ((wanted >> bit) & 1) << place
    return jnp.take(held, slot, axis=0, mode="clip")


def gather_rows(rows, axis):
    bits = lax.axis_size(axis).bit_length() - 1
    upper = list(range(1, bits))
    half = rows.shape[0] // 2
    first = exchange_gather(rows[:half], axis, upper + [0] if bits else [])
    second = exchange_gather(rows[half:], axis, upper[::-1] + [0] if bits else [])
    return jnp.concatenate([first, second], axis=1).reshape((-1,) + rows.shape[1:])


def shards(tokens, query_weight, keyval_matrix, grad_out, blocks, counts):
    local_rows = tokens[0]
    dp_size = lax.axis_size("dp")
    row_block = local_rows.shape[1] // dp_size
    row_slices = lax.all_to_all(
        local_rows.reshape(local_rows.shape[0], dp_size, row_block).transpose(1, 0, 2),
        "dp", split_axis=0, concat_axis=0, tiled=True,
    )
    group_size = lax.axis_size("ctx") // blocks.shape[0]
    group_bits = group_size.bit_length() - 1
    device = lax.axis_index("ctx")
    query_cols = query_weight.shape[1]
    weights_full = lax.all_gather(
        jnp.concatenate([query_weight, keyval_matrix], axis=1), "dp", axis=0, tiled=True
    )
    query_full = weights_full[:, :query_cols]
    keyval_part = weights_full[:, query_cols:]
    all_rows = gather_rows(local_rows, "ctx")
    all_rows, row_slices = lax.optimization_barrier((all_rows, row_slices))
    keyval_cols = keyval_part
    for bit in range(group_bits):
        other = partner(keyval_cols, "ctx", bit)
        upper = device >> bit & 1 == 1
        keyval_cols = jnp.where(
            upper,
            jnp.concatenate([other, keyval_cols], axis=1),
            jnp.concatenate([keyval_cols, other], axis=1),
        )
    projected = jnp.dot(
        all_rows,
        jnp.concatenate([query_full, keyval_cols], axis=1),
        preferred_element_type=jnp.float32,
    ).astype(jnp.bfloat16)
    q_heads = projected[:, :query_cols]
    keyval_rows = projected[:, query_cols:]
    dout_heads = lax.all_to_all(grad_out[0], "ctx", split_axis=1, concat_axis=0, tiled=True)
    group_index = device // group_size
    blk = lax.dynamic_index_in_dim(blocks, group_index, 0, keepdims=False)
    cnt = lax.dynamic_index_in_dim(counts, group_index, 0, keepdims=False)
    out_heads, dquery, keyval_grad = attention(q_heads, keyval_rows, dout_heads, blk, cnt)
    attended = lax.all_to_all(out_heads, "ctx", split_axis=0, concat_axis=1, tiled=True)
    summed = keyval_grad
    for bit in range(group_bits):
        summed = summed + partner(summed, "ctx", bit)
    width = summed.shape[1] // group_size
    own_grad = lax.dynamic_slice_in_dim(summed, device % group_size * width, width, 1)
    own_grad = own_grad.astype(jnp.bfloat16)
    row_tokens = lax.all_gather(row_slices, "ctx", axis=1, tiled=True)
    row_tokens, dquery = lax.optimization_barrier((row_tokens, dquery))
    query_cot = lax.all_gather(dquery, "dp", axis=0, tiled=False)
    grad_query = jnp.einsum(
        "spr,spk->rk", row_tokens, query_cot, preferred_element_type=jnp.float32
    )
    keyval_cot = lax.all_gather(own_grad, "dp", axis=0, tiled=False)
    grad_keyval = jnp.einsum(
        "spr,spk->rk", row_tokens, keyval_cot, preferred_element_type=jnp.float32
    )
    return (attended[None], grad_query, grad_keyval)


def solution(mesh):
    in_specs = (
        P("dp", "ctx", None),
        P("dp", "ctx"),
        P("dp", "ctx"),
        P("dp", "ctx", None),
        P(),
        P(),
    )
    out_specs = (P("dp", "ctx", None), P("dp", "ctx"), P("dp", "ctx"))
    return jax.shard_map(shards, mesh=mesh, in_specs=in_specs, out_specs=out_specs, check_vma=False)
```

```python
import jax
import jax.numpy as jnp
from jax import lax
from jax.sharding import PartitionSpec as P


def partner(block, axis, distance):
    count = lax.axis_size(axis)
    route = []
    for low in range(count):
        high = low | 1 << distance
        if high != low and high < count:
            route += [(low, high), (high, low)]
    return lax.ppermute(block, axis, route)


def attend_part(query_rows, key_rows, vals, dout, valid, scale):
    scores = (
        jnp.einsum("nqhd,nkcd->nhqkc", query_rows, key_rows, preferred_element_type=jnp.float32)
        * scale
    )
    scores = jnp.where(valid[:, None, None, :, None], scores, -jnp.inf)
    peak = jnp.max(scores, axis=(3, 4), keepdims=True)
    expo = jnp.exp(scores - peak)
    probs = expo / jnp.sum(expo, axis=(3, 4), keepdims=True)
    probs_b = probs.astype(jnp.bfloat16)
    out = jnp.einsum("nhqkc,nkcd->nqhd", probs_b, vals, preferred_element_type=jnp.float32).astype(
        jnp.bfloat16
    )
    delta = jnp.transpose(
        jnp.sum(dout.astype(jnp.float32) * out.astype(jnp.float32), axis=3), (0, 2, 1)
    )
    dprob = jnp.einsum("nqhd,nkcd->nhqkc", dout, vals, preferred_element_type=jnp.float32)
    dscore = (probs * (dprob - delta[:, :, :, None, None]) * scale).astype(jnp.bfloat16)
    dquery = jnp.einsum(
        "nhqkc,nkcd->nqhd", dscore, key_rows, preferred_element_type=jnp.float32
    ).astype(jnp.bfloat16)
    dkeys = jnp.einsum("nhqkc,nqhd->nkcd", dscore, query_rows, preferred_element_type=jnp.float32)
    dvals = jnp.einsum("nhqkc,nqhd->nkcd", probs_b, dout, preferred_element_type=jnp.float32)
    return (out, dquery, dkeys, dvals)


def attention(q_heads, keyval_rows, dout_heads, blk, cnt):
    length = q_heads.shape[0]
    head_size = keyval_rows.shape[1] // 2
    heads = q_heads.shape[1] // head_size
    nblocks, kslots = blk.shape
    block = length // nblocks
    scale = head_size ** (-0.5)
    step = 4
    groups = nblocks // step
    key_rows = keyval_rows[:, :head_size].reshape(nblocks, block, head_size)
    vals = keyval_rows[:, head_size:].reshape(nblocks, block, head_size)
    valid = lax.broadcasted_iota(jnp.int32, (nblocks, kslots), 1) < cnt[:, None]
    query_rows = q_heads.reshape(groups, step, block, heads, head_size)
    dout = dout_heads.reshape(groups, step, block, heads, head_size)

    def one_step(args):
        q_part, d_part, b_part, v_part = args
        return attend_part(q_part, key_rows[b_part], vals[b_part], d_part, v_part, scale)

    out, dquery, dkeys, dvals = lax.map(
        one_step,
        (query_rows, dout, blk.reshape(groups, step, kslots), valid.reshape(groups, step, kslots)),
    )
    return (
        out.reshape(length, heads * head_size),
        dquery.reshape(length, heads * head_size),
        (dkeys, dvals),
    )


def scatter_slots(dkeys, dvals, blk, cnt):
    nblocks, kslots = blk.shape
    block, head_size = dkeys.shape[-2:]
    length = nblocks * block
    valid = lax.broadcasted_iota(jnp.int32, (nblocks, kslots), 1) < cnt[:, None]
    dkeys = dkeys.reshape(nblocks, kslots, block, head_size)
    dvals = dvals.reshape(nblocks, kslots, block, head_size)
    onehot = (
        (blk[None, :, :] == lax.broadcasted_iota(jnp.int32, (nblocks, 1, 1), 0)) & valid[None]
    ).astype(jnp.float32)
    key_grad = jnp.einsum("bnk,nkcd->bcd", onehot, dkeys, precision=lax.Precision.HIGHEST)
    val_grad = jnp.einsum("bnk,nkcd->bcd", onehot, dvals, precision=lax.Precision.HIGHEST)
    keyval_grad = jnp.concatenate(
        [key_grad.reshape(length, head_size), val_grad.reshape(length, head_size)], axis=1
    )
    return keyval_grad


def exchange_gather(block, axis, order):
    count = lax.axis_size(axis)
    held = block[None]
    for bit in order:
        held = jnp.concatenate([held, partner(held, axis, bit)], axis=0)
    wanted = lax.broadcasted_iota(jnp.int32, (count,), 0) ^ lax.axis_index(axis)
    slot = jnp.zeros((count,), jnp.int32)
    for place, bit in enumerate(order):
        slot = slot | ((wanted >> bit) & 1) << place
    return jnp.take(held, slot, axis=0, mode="clip")


def gather_rows(rows, axis):
    bits = lax.axis_size(axis).bit_length() - 1
    upper = list(range(1, bits))
    half = rows.shape[0] // 2
    first = exchange_gather(rows[:half], axis, upper + [0] if bits else [])
    second = exchange_gather(rows[half:], axis, upper[::-1] + [0] if bits else [])
    return jnp.concatenate([first, second], axis=1).reshape((-1,) + rows.shape[1:])


def shards(tokens, query_weight, keyval_matrix, grad_out, blocks, counts):
    local_rows = tokens[0]
    dp_size = lax.axis_size("dp")
    row_block = local_rows.shape[1] // dp_size
    row_slices = lax.all_to_all(
        local_rows.reshape(local_rows.shape[0], dp_size, row_block).transpose(1, 0, 2),
        "dp", split_axis=0, concat_axis=0, tiled=True,
    )
    group_size = lax.axis_size("ctx") // blocks.shape[0]
    group_bits = group_size.bit_length() - 1
    device = lax.axis_index("ctx")
    query_cols = query_weight.shape[1]
    weights_full = lax.all_gather(
        jnp.concatenate([query_weight, keyval_matrix], axis=1), "dp", axis=0, tiled=True
    )
    query_full = weights_full[:, :query_cols]
    keyval_part = weights_full[:, query_cols:]
    all_rows = gather_rows(local_rows, "ctx")
    all_rows, row_slices = lax.optimization_barrier((all_rows, row_slices))
    keyval_cols = keyval_part
    for bit in range(group_bits):
        other = partner(keyval_cols, "ctx", bit)
        upper = device >> bit & 1 == 1
        keyval_cols = jnp.where(
            upper,
            jnp.concatenate([other, keyval_cols], axis=1),
            jnp.concatenate([keyval_cols, other], axis=1),
        )
    projected = jnp.dot(
        all_rows,
        jnp.concatenate([query_full, keyval_cols], axis=1),
        preferred_element_type=jnp.float32,
    ).astype(jnp.bfloat16)
    q_heads = projected[:, :query_cols]
    keyval_rows = projected[:, query_cols:]
    dout_heads = lax.all_to_all(grad_out[0], "ctx", split_axis=1, concat_axis=0, tiled=True)
    group_index = device // group_size
    blk = lax.dynamic_index_in_dim(blocks, group_index, 0, keepdims=False)
    cnt = lax.dynamic_index_in_dim(counts, group_index, 0, keepdims=False)
    head_size = keyval_rows.shape[1] // 2
    heads = query_cols // head_size
    chunks = 2 if heads % 2 == 0 else 1
    chunk_cols = query_cols // chunks
    row_tokens = lax.all_gather(row_slices, "ctx", axis=1, tiled=True)
    outs, partials, grads = [], None, []
    for k in range(chunks):
        cols = slice(k * chunk_cols, (k + 1) * chunk_cols)
        out_part, dquery, part = attention(
            q_heads[:, cols], keyval_rows, dout_heads[:, cols], blk, cnt
        )
        if k == 0:
            row_tokens, dquery = lax.optimization_barrier((row_tokens, dquery))
        else:
            cotangents, dquery = lax.optimization_barrier((cotangents, dquery))
            grads.append(
                jnp.einsum("spr,spk->rk", row_tokens, cotangents, preferred_element_type=jnp.float32)
            )
        outs.append(out_part)
        partials = part if partials is None else (partials[0] + part[0], partials[1] + part[1])
        if k == chunks - 1:
            summed = scatter_slots(partials[0], partials[1], blk, cnt)
            for bit in range(group_bits):
                summed = summed + partner(summed, "ctx", bit)
            width = summed.shape[1] // group_size
            own_grad = lax.dynamic_slice_in_dim(summed, device % group_size * width, width, 1)
            dquery = jnp.concatenate([dquery, own_grad.astype(jnp.bfloat16)], axis=1)
        cotangents = lax.all_gather(dquery, "dp", axis=0, tiled=False)
    grads.append(
        jnp.einsum("spr,spk->rk", row_tokens, cotangents, preferred_element_type=jnp.float32)
    )
    attended = lax.all_to_all(
        jnp.concatenate(outs, axis=1), "ctx", split_axis=0, concat_axis=1, tiled=True
    )
    grads = jnp.concatenate(grads, axis=1)
    grad_query = grads[:, :query_cols]
    grad_keyval = grads[:, query_cols:]
    return (attended[None], grad_query, grad_keyval)


def solution(mesh):
    in_specs = (
        P("dp", "ctx", None),
        P("dp", "ctx"),
        P("dp", "ctx"),
        P("dp", "ctx", None),
        P(),
        P(),
    )
    out_specs = (P("dp", "ctx", None), P("dp", "ctx"), P("dp", "ctx"))
    return jax.shard_map(shards, mesh=mesh, in_specs=in_specs, out_specs=out_specs, check_vma=False)
```

```python
import jax
import jax.numpy as jnp
from jax import lax
from jax.sharding import PartitionSpec as P


def partner(block, axis, distance):
    count = lax.axis_size(axis)
    route = []
    for low in range(count):
        high = low | 1 << distance
        if high != low and high < count:
            route += [(low, high), (high, low)]
    return lax.ppermute(block, axis, route)


def attend_part(query_rows, key_rows, vals, dout, valid, scale):
    scores = (
        jnp.einsum("nqhd,nkcd->nhqkc", query_rows, key_rows, preferred_element_type=jnp.float32)
        * scale
    )
    scores = jnp.where(valid[:, None, None, :, None], scores, -jnp.inf)
    peak = jnp.max(scores, axis=(3, 4), keepdims=True)
    expo = jnp.exp(scores - peak)
    probs = expo / jnp.sum(expo, axis=(3, 4), keepdims=True)
    probs_b = probs.astype(jnp.bfloat16)
    out = jnp.einsum("nhqkc,nkcd->nqhd", probs_b, vals, preferred_element_type=jnp.float32).astype(
        jnp.bfloat16
    )
    delta = jnp.transpose(
        jnp.sum(dout.astype(jnp.float32) * out.astype(jnp.float32), axis=3), (0, 2, 1)
    )
    dprob = jnp.einsum("nqhd,nkcd->nhqkc", dout, vals, preferred_element_type=jnp.float32)
    dscore = (probs * (dprob - delta[:, :, :, None, None]) * scale).astype(jnp.bfloat16)
    dquery = jnp.einsum(
        "nhqkc,nkcd->nqhd", dscore, key_rows, preferred_element_type=jnp.float32
    ).astype(jnp.bfloat16)
    dkeys = jnp.einsum("nhqkc,nqhd->nkcd", dscore, query_rows, preferred_element_type=jnp.float32)
    dvals = jnp.einsum("nhqkc,nqhd->nkcd", probs_b, dout, preferred_element_type=jnp.float32)
    return (out, dquery, dkeys, dvals)


def attention(q_heads, keyval_rows, dout_heads, blk, cnt):
    length = q_heads.shape[0]
    head_size = keyval_rows.shape[1] // 2
    heads = q_heads.shape[1] // head_size
    nblocks, kslots = blk.shape
    block = length // nblocks
    scale = head_size ** (-0.5)
    step = 4
    groups = nblocks // step
    key_rows = keyval_rows[:, :head_size].reshape(nblocks, block, head_size)
    vals = keyval_rows[:, head_size:].reshape(nblocks, block, head_size)
    valid = lax.broadcasted_iota(jnp.int32, (nblocks, kslots), 1) < cnt[:, None]
    query_rows = q_heads.reshape(groups, step, block, heads, head_size)
    dout = dout_heads.reshape(groups, step, block, heads, head_size)

    def one_step(args):
        q_part, d_part, b_part, v_part = args
        return attend_part(q_part, key_rows[b_part], vals[b_part], d_part, v_part, scale)

    out, dquery, dkeys, dvals = lax.map(
        one_step,
        (query_rows, dout, blk.reshape(groups, step, kslots), valid.reshape(groups, step, kslots)),
    )
    return (
        out.reshape(length, heads * head_size),
        dquery.reshape(length, heads * head_size),
        (dkeys, dvals),
    )


def scatter_slots(dkeys, dvals, blk, cnt):
    nblocks, kslots = blk.shape
    block, head_size = dkeys.shape[-2:]
    length = nblocks * block
    valid = lax.broadcasted_iota(jnp.int32, (nblocks, kslots), 1) < cnt[:, None]
    dkeys = dkeys.reshape(nblocks, kslots, block, head_size)
    dvals = dvals.reshape(nblocks, kslots, block, head_size)
    onehot = (
        (blk[None, :, :] == lax.broadcasted_iota(jnp.int32, (nblocks, 1, 1), 0)) & valid[None]
    ).astype(jnp.float32)
    key_grad = jnp.einsum("bnk,nkcd->bcd", onehot, dkeys, precision=lax.Precision.HIGHEST)
    val_grad = jnp.einsum("bnk,nkcd->bcd", onehot, dvals, precision=lax.Precision.HIGHEST)
    keyval_grad = jnp.concatenate(
        [key_grad.reshape(length, head_size), val_grad.reshape(length, head_size)], axis=1
    )
    return keyval_grad


def exchange_gather(block, axis, order):
    count = lax.axis_size(axis)
    held = block[None]
    for bit in order:
        held = jnp.concatenate([held, partner(held, axis, bit)], axis=0)
    wanted = lax.broadcasted_iota(jnp.int32, (count,), 0) ^ lax.axis_index(axis)
    slot = jnp.zeros((count,), jnp.int32)
    for place, bit in enumerate(order):
        slot = slot | ((wanted >> bit) & 1) << place
    return jnp.take(held, slot, axis=0, mode="clip")


def gather_rows(rows, axis):
    bits = lax.axis_size(axis).bit_length() - 1
    upper = list(range(1, bits))
    half = rows.shape[0] // 2
    first = exchange_gather(rows[:half], axis, upper + [0] if bits else [])
    second = exchange_gather(rows[half:], axis, upper[::-1] + [0] if bits else [])
    return jnp.concatenate([first, second], axis=1).reshape((-1,) + rows.shape[1:])


def shards(tokens, query_weight, keyval_matrix, grad_out, blocks, counts):
    local_rows = tokens[0]
    dp_size = lax.axis_size("dp")
    row_block = local_rows.shape[1] // dp_size
    row_slices = lax.all_to_all(
        local_rows.reshape(local_rows.shape[0], dp_size, row_block).transpose(1, 0, 2),
        "dp", split_axis=0, concat_axis=0, tiled=True,
    )
    group_size = lax.axis_size("ctx") // blocks.shape[0]
    group_bits = group_size.bit_length() - 1
    device = lax.axis_index("ctx")
    query_cols = query_weight.shape[1]
    head_size = keyval_matrix.shape[1] * group_size // 2
    chunks = 2 if query_cols // head_size % 2 == 0 else 1
    chunk_cols = query_cols // chunks
    weights_first = lax.all_gather(
        jnp.concatenate([query_weight[:, :chunk_cols], keyval_matrix], axis=1),
        "dp", axis=0, tiled=True,
    )
    later_weights = [
        lax.all_gather(query_weight[:, k * chunk_cols:(k + 1) * chunk_cols], "dp", axis=0, tiled=True)
        for k in range(1, chunks)
    ]
    query_first = weights_first[:, :chunk_cols]
    keyval_part = weights_first[:, chunk_cols:]
    all_rows = gather_rows(local_rows, "ctx")
    all_rows, row_slices = lax.optimization_barrier((all_rows, row_slices))
    keyval_cols = keyval_part
    for bit in range(group_bits):
        other = partner(keyval_cols, "ctx", bit)
        upper = device >> bit & 1 == 1
        keyval_cols = jnp.where(
            upper,
            jnp.concatenate([other, keyval_cols], axis=1),
            jnp.concatenate([keyval_cols, other], axis=1),
        )
    projected = jnp.dot(
        all_rows,
        jnp.concatenate([query_first, keyval_cols], axis=1),
        preferred_element_type=jnp.float32,
    ).astype(jnp.bfloat16)
    q_chunks = [projected[:, :chunk_cols]]
    keyval_rows = projected[:, chunk_cols:]
    dout_heads = lax.all_to_all(grad_out[0], "ctx", split_axis=1, concat_axis=0, tiled=True)
    group_index = device // group_size
    blk = lax.dynamic_index_in_dim(blocks, group_index, 0, keepdims=False)
    cnt = lax.dynamic_index_in_dim(counts, group_index, 0, keepdims=False)
    row_tokens = lax.all_gather(row_slices, "ctx", axis=1, tiled=True)
    outs, partials, grads = [], None, []
    for k in range(chunks):
        cols = slice(k * chunk_cols, (k + 1) * chunk_cols)
        if k:
            q_chunks.append(
                jnp.dot(all_rows, later_weights[k - 1], preferred_element_type=jnp.float32).astype(
                    jnp.bfloat16
                )
            )
        out_part, dquery, part = attention(
            q_chunks[k], keyval_rows, dout_heads[:, cols], blk, cnt
        )
        if k < chunks - 1:
            later_weights[k], dquery = lax.optimization_barrier((later_weights[k], dquery))
        if k == 0:
            row_tokens, dquery = lax.optimization_barrier((row_tokens, dquery))
        else:
            cotangents, dquery = lax.optimization_barrier((cotangents, dquery))
            grads.append(
                jnp.einsum("spr,spk->rk", row_tokens, cotangents, preferred_element_type=jnp.float32)
            )
        outs.append(out_part)
        partials = part if partials is None else (partials[0] + part[0], partials[1] + part[1])
        if k == chunks - 1:
            summed = scatter_slots(partials[0], partials[1], blk, cnt)
            for bit in range(group_bits):
                summed = summed + partner(summed, "ctx", bit)
            width = summed.shape[1] // group_size
            own_grad = lax.dynamic_slice_in_dim(summed, device % group_size * width, width, 1)
            dquery = jnp.concatenate([dquery, own_grad.astype(jnp.bfloat16)], axis=1)
        cotangents = lax.all_gather(dquery, "dp", axis=0, tiled=False)
    grads.append(
        jnp.einsum("spr,spk->rk", row_tokens, cotangents, preferred_element_type=jnp.float32)
    )
    attended = lax.all_to_all(
        jnp.concatenate(outs, axis=1), "ctx", split_axis=0, concat_axis=1, tiled=True
    )
    grads = jnp.concatenate(grads, axis=1)
    grad_query = grads[:, :query_cols]
    grad_keyval = grads[:, query_cols:]
    return (attended[None], grad_query, grad_keyval)


def solution(mesh):
    in_specs = (
        P("dp", "ctx", None),
        P("dp", "ctx"),
        P("dp", "ctx"),
        P("dp", "ctx", None),
        P(),
        P(),
    )
    out_specs = (P("dp", "ctx", None), P("dp", "ctx"), P("dp", "ctx"))
    return jax.shard_map(shards, mesh=mesh, in_specs=in_specs, out_specs=out_specs, check_vma=False)
```

```python
import jax
import jax.numpy as jnp
from jax import lax
from jax.sharding import PartitionSpec as P


def partner(block, axis, distance):
    count = lax.axis_size(axis)
    route = []
    for low in range(count):
        high = low | 1 << distance
        if high != low and high < count:
            route += [(low, high), (high, low)]
    return lax.ppermute(block, axis, route)


def attend_part(query_rows, key_rows, vals, dout, valid, scale):
    scores = (
        jnp.einsum("nqhd,nkcd->nhqkc", query_rows, key_rows, preferred_element_type=jnp.float32)
        * scale
    )
    scores = jnp.where(valid[:, None, None, :, None], scores, -jnp.inf)
    peak = jnp.max(scores, axis=(3, 4), keepdims=True)
    expo = jnp.exp(scores - peak)
    probs = expo / jnp.sum(expo, axis=(3, 4), keepdims=True)
    probs_b = probs.astype(jnp.bfloat16)
    out = jnp.einsum("nhqkc,nkcd->nqhd", probs_b, vals, preferred_element_type=jnp.float32).astype(
        jnp.bfloat16
    )
    delta = jnp.transpose(
        jnp.sum(dout.astype(jnp.float32) * out.astype(jnp.float32), axis=3), (0, 2, 1)
    )
    dprob = jnp.einsum("nqhd,nkcd->nhqkc", dout, vals, preferred_element_type=jnp.float32)
    dscore = (probs * (dprob - delta[:, :, :, None, None]) * scale).astype(jnp.bfloat16)
    dquery = jnp.einsum(
        "nhqkc,nkcd->nqhd", dscore, key_rows, preferred_element_type=jnp.float32
    ).astype(jnp.bfloat16)
    dkeys = jnp.einsum("nhqkc,nqhd->nkcd", dscore, query_rows, preferred_element_type=jnp.float32)
    dvals = jnp.einsum("nhqkc,nqhd->nkcd", probs_b, dout, preferred_element_type=jnp.float32)
    return (out, dquery, dkeys, dvals)


def attention(q_heads, keyval_rows, dout_heads, blk, cnt):
    length = q_heads.shape[0]
    head_size = keyval_rows.shape[1] // 2
    heads = q_heads.shape[1] // head_size
    nblocks, kslots = blk.shape
    block = length // nblocks
    scale = head_size ** (-0.5)
    step = 4
    groups = nblocks // step
    key_rows = keyval_rows[:, :head_size].reshape(nblocks, block, head_size)
    vals = keyval_rows[:, head_size:].reshape(nblocks, block, head_size)
    valid = lax.broadcasted_iota(jnp.int32, (nblocks, kslots), 1) < cnt[:, None]
    query_rows = q_heads.reshape(groups, step, block, heads, head_size)
    dout = dout_heads.reshape(groups, step, block, heads, head_size)

    def one_step(args):
        q_part, d_part, b_part, v_part = args
        return attend_part(q_part, key_rows[b_part], vals[b_part], d_part, v_part, scale)

    out, dquery, dkeys, dvals = lax.map(
        one_step,
        (query_rows, dout, blk.reshape(groups, step, kslots), valid.reshape(groups, step, kslots)),
    )
    return (
        out.reshape(length, heads * head_size),
        dquery.reshape(length, heads * head_size),
        (dkeys, dvals),
    )


def scatter_slots(dkeys, dvals, blk, cnt):
    nblocks, kslots = blk.shape
    block, head_size = dkeys.shape[-2:]
    length = nblocks * block
    valid = lax.broadcasted_iota(jnp.int32, (nblocks, kslots), 1) < cnt[:, None]
    dkeys = dkeys.reshape(nblocks, kslots, block, head_size)
    dvals = dvals.reshape(nblocks, kslots, block, head_size)
    onehot = (
        (blk[None, :, :] == lax.broadcasted_iota(jnp.int32, (nblocks, 1, 1), 0)) & valid[None]
    ).astype(jnp.float32)
    key_grad = jnp.einsum("bnk,nkcd->bcd", onehot, dkeys, precision=lax.Precision.HIGHEST)
    val_grad = jnp.einsum("bnk,nkcd->bcd", onehot, dvals, precision=lax.Precision.HIGHEST)
    keyval_grad = jnp.concatenate(
        [key_grad.reshape(length, head_size), val_grad.reshape(length, head_size)], axis=1
    )
    return keyval_grad


def exchange_gather(block, axis, order):
    count = lax.axis_size(axis)
    held = block[None]
    for bit in order:
        held = jnp.concatenate([held, partner(held, axis, bit)], axis=0)
    wanted = lax.broadcasted_iota(jnp.int32, (count,), 0) ^ lax.axis_index(axis)
    slot = jnp.zeros((count,), jnp.int32)
    for place, bit in enumerate(order):
        slot = slot | ((wanted >> bit) & 1) << place
    return held, slot


def gather_rows(rows, axis):
    bits = lax.axis_size(axis).bit_length() - 1
    upper = list(range(1, bits))
    half = rows.shape[0] // 2
    return [
        exchange_gather(rows[:half], axis, upper + [0] if bits else []),
        exchange_gather(rows[half:], axis, upper[::-1] + [0] if bits else []),
    ]


def project(halves, weights):
    parts = []
    for held, slot in halves:
        product = jnp.dot(
            held.reshape(-1, held.shape[-1]), weights, preferred_element_type=jnp.float32
        ).astype(jnp.bfloat16)
        product = product.reshape(held.shape[:2] + (weights.shape[1],))
        parts.append(jnp.take(product, slot, axis=0, mode="clip"))
    return jnp.concatenate(parts, axis=1).reshape(-1, weights.shape[1])


def shards(tokens, query_weight, keyval_matrix, grad_out, blocks, counts):
    local_rows = tokens[0]
    dp_size = lax.axis_size("dp")
    row_block = local_rows.shape[1] // dp_size
    row_slices = lax.all_to_all(
        local_rows.reshape(local_rows.shape[0], dp_size, row_block).transpose(1, 0, 2),
        "dp", split_axis=0, concat_axis=0, tiled=True,
    )
    group_size = lax.axis_size("ctx") // blocks.shape[0]
    group_bits = group_size.bit_length() - 1
    device = lax.axis_index("ctx")
    query_cols = query_weight.shape[1]
    head_size = keyval_matrix.shape[1] * group_size // 2
    chunks = 2 if query_cols // head_size % 2 == 0 else 1
    chunk_cols = query_cols // chunks
    weights_first = lax.all_gather(
        jnp.concatenate([query_weight[:, :chunk_cols], keyval_matrix], axis=1),
        "dp", axis=0, tiled=True,
    )
    later_weights = [
        lax.all_gather(query_weight[:, k * chunk_cols:(k + 1) * chunk_cols], "dp", axis=0, tiled=True)
        for k in range(1, chunks)
    ]
    query_first = weights_first[:, :chunk_cols]
    keyval_part = weights_first[:, chunk_cols:]
    all_rows = gather_rows(local_rows, "ctx")
    all_rows, row_slices = lax.optimization_barrier((all_rows, row_slices))
    all_rows = [(held, slot) for held, slot in all_rows]
    keyval_cols = keyval_part
    for bit in range(group_bits):
        other = partner(keyval_cols, "ctx", bit)
        upper = device >> bit & 1 == 1
        keyval_cols = jnp.where(
            upper,
            jnp.concatenate([other, keyval_cols], axis=1),
            jnp.concatenate([keyval_cols, other], axis=1),
        )
    projected = project(all_rows, jnp.concatenate([query_first, keyval_cols], axis=1))
    q_chunks = [projected[:, :chunk_cols]]
    keyval_rows = projected[:, chunk_cols:]
    dout_heads = lax.all_to_all(grad_out[0], "ctx", split_axis=1, concat_axis=0, tiled=True)
    group_index = device // group_size
    blk = lax.dynamic_index_in_dim(blocks, group_index, 0, keepdims=False)
    cnt = lax.dynamic_index_in_dim(counts, group_index, 0, keepdims=False)
    row_tokens = lax.all_gather(row_slices, "ctx", axis=1, tiled=True)
    outs, partials, grads = [], None, []
    for k in range(chunks):
        cols = slice(k * chunk_cols, (k + 1) * chunk_cols)
        if k:
            q_chunks.append(project(all_rows, later_weights[k - 1]))
        out_part, dquery, part = attention(
            q_chunks[k], keyval_rows, dout_heads[:, cols], blk, cnt
        )
        if k < chunks - 1:
            later_weights[k], dquery = lax.optimization_barrier((later_weights[k], dquery))
        if k == 0:
            row_tokens, dquery = lax.optimization_barrier((row_tokens, dquery))
        else:
            cotangents, dquery = lax.optimization_barrier((cotangents, dquery))
            grads.append(
                jnp.einsum("spr,spk->rk", row_tokens, cotangents, preferred_element_type=jnp.float32)
            )
        outs.append(out_part)
        partials = part if partials is None else (partials[0] + part[0], partials[1] + part[1])
        if k == chunks - 1:
            summed = scatter_slots(partials[0], partials[1], blk, cnt)
            for bit in range(group_bits):
                summed = summed + partner(summed, "ctx", bit)
            width = summed.shape[1] // group_size
            own_grad = lax.dynamic_slice_in_dim(summed, device % group_size * width, width, 1)
            dquery = jnp.concatenate([dquery, own_grad.astype(jnp.bfloat16)], axis=1)
        cotangents = lax.all_gather(dquery, "dp", axis=0, tiled=False)
    grads.append(
        jnp.einsum("spr,spk->rk", row_tokens, cotangents, preferred_element_type=jnp.float32)
    )
    attended = lax.all_to_all(
        jnp.concatenate(outs, axis=1), "ctx", split_axis=0, concat_axis=1, tiled=True
    )
    grads = jnp.concatenate(grads, axis=1)
    grad_query = grads[:, :query_cols]
    grad_keyval = grads[:, query_cols:]
    return (attended[None], grad_query, grad_keyval)


def solution(mesh):
    in_specs = (
        P("dp", "ctx", None),
        P("dp", "ctx"),
        P("dp", "ctx"),
        P("dp", "ctx", None),
        P(),
        P(),
    )
    out_specs = (P("dp", "ctx", None), P("dp", "ctx"), P("dp", "ctx"))
    return jax.shard_map(shards, mesh=mesh, in_specs=in_specs, out_specs=out_specs, check_vma=False)
```

```python
import jax
import jax.numpy as jnp
from jax import lax
from jax.sharding import PartitionSpec as P


def partner(block, axis, distance):
    count = lax.axis_size(axis)
    route = []
    for low in range(count):
        high = low | 1 << distance
        if high != low and high < count:
            route += [(low, high), (high, low)]
    return lax.ppermute(block, axis, route)


def attend_part(query_rows, key_rows, vals, dout, valid, scale):
    scores = (
        jnp.einsum("nqhd,nkcd->nhqkc", query_rows, key_rows, preferred_element_type=jnp.float32)
        * scale
    )
    scores = jnp.where(valid[:, None, None, :, None], scores, -jnp.inf)
    peak = jnp.max(scores, axis=(3, 4), keepdims=True)
    expo = jnp.exp(scores - peak)
    probs = expo / jnp.sum(expo, axis=(3, 4), keepdims=True)
    probs_b = probs.astype(jnp.bfloat16)
    out = jnp.einsum("nhqkc,nkcd->nqhd", probs_b, vals, preferred_element_type=jnp.float32).astype(
        jnp.bfloat16
    )
    delta = jnp.transpose(
        jnp.sum(dout.astype(jnp.float32) * out.astype(jnp.float32), axis=3), (0, 2, 1)
    )
    dprob = jnp.einsum("nqhd,nkcd->nhqkc", dout, vals, preferred_element_type=jnp.float32)
    dscore = (probs * (dprob - delta[:, :, :, None, None]) * scale).astype(jnp.bfloat16)
    dquery = jnp.einsum(
        "nhqkc,nkcd->nqhd", dscore, key_rows, preferred_element_type=jnp.float32
    ).astype(jnp.bfloat16)
    dkeys = jnp.einsum("nhqkc,nqhd->nkcd", dscore, query_rows, preferred_element_type=jnp.float32)
    dvals = jnp.einsum("nhqkc,nqhd->nkcd", probs_b, dout, preferred_element_type=jnp.float32)
    return (out, dquery, dkeys, dvals)


def attention(q_heads, keyval_rows, dout_heads, blk, cnt):
    length = q_heads.shape[0]
    head_size = keyval_rows.shape[1] // 2
    heads = q_heads.shape[1] // head_size
    nblocks, kslots = blk.shape
    block = length // nblocks
    scale = head_size ** (-0.5)
    step = 4
    groups = nblocks // step
    key_rows = keyval_rows[:, :head_size].reshape(nblocks, block, head_size)
    vals = keyval_rows[:, head_size:].reshape(nblocks, block, head_size)
    valid = lax.broadcasted_iota(jnp.int32, (nblocks, kslots), 1) < cnt[:, None]
    query_rows = q_heads.reshape(groups, step, block, heads, head_size)
    dout = dout_heads.reshape(groups, step, block, heads, head_size)

    def one_step(args):
        q_part, d_part, b_part, v_part = args
        return attend_part(q_part, key_rows[b_part], vals[b_part], d_part, v_part, scale)

    out, dquery, dkeys, dvals = lax.map(
        one_step,
        (query_rows, dout, blk.reshape(groups, step, kslots), valid.reshape(groups, step, kslots)),
    )
    return (
        out.reshape(length, heads * head_size),
        dquery.reshape(length, heads * head_size),
        (dkeys, dvals),
    )


def scatter_slots(dkeys, dvals, blk, cnt):
    nblocks, kslots = blk.shape
    block, head_size = dkeys.shape[-2:]
    length = nblocks * block
    valid = lax.broadcasted_iota(jnp.int32, (nblocks, kslots), 1) < cnt[:, None]
    dkeys = dkeys.reshape(nblocks, kslots, block, head_size)
    dvals = dvals.reshape(nblocks, kslots, block, head_size)
    onehot = (
        (blk[None, :, :] == lax.broadcasted_iota(jnp.int32, (nblocks, 1, 1), 0)) & valid[None]
    ).astype(jnp.float32)
    key_grad = jnp.einsum("bnk,nkcd->bcd", onehot, dkeys, precision=lax.Precision.HIGHEST)
    val_grad = jnp.einsum("bnk,nkcd->bcd", onehot, dvals, precision=lax.Precision.HIGHEST)
    keyval_grad = jnp.concatenate(
        [key_grad.reshape(length, head_size), val_grad.reshape(length, head_size)], axis=1
    )
    return keyval_grad


def exchange_gather(block, axis, order):
    count = lax.axis_size(axis)
    held = block[None]
    for bit in order:
        held = jnp.concatenate([held, partner(held, axis, bit)], axis=0)
    wanted = lax.broadcasted_iota(jnp.int32, (count,), 0) ^ lax.axis_index(axis)
    slot = jnp.zeros((count,), jnp.int32)
    for place, bit in enumerate(order):
        slot = slot | ((wanted >> bit) & 1) << place
    return jnp.take(held, slot, axis=0, mode="clip")


def gather_rows(rows, axis):
    bits = lax.axis_size(axis).bit_length() - 1
    upper = list(range(1, bits))
    half = rows.shape[0] // 2
    first = exchange_gather(rows[:half], axis, upper + [0] if bits else [])
    second = exchange_gather(rows[half:], axis, upper[::-1] + [0] if bits else [])
    return jnp.concatenate([first, second], axis=1).reshape((-1,) + rows.shape[1:])


def shards(tokens, query_weight, keyval_matrix, grad_out, blocks, counts):
    local_rows = tokens[0]
    dp_size = lax.axis_size("dp")
    row_block = local_rows.shape[1] // dp_size
    row_slices = lax.all_to_all(
        local_rows.reshape(local_rows.shape[0], dp_size, row_block).transpose(1, 0, 2),
        "dp", split_axis=0, concat_axis=0, tiled=True,
    )
    group_size = lax.axis_size("ctx") // blocks.shape[0]
    group_bits = group_size.bit_length() - 1
    device = lax.axis_index("ctx")
    query_cols = query_weight.shape[1]
    head_size = keyval_matrix.shape[1] * group_size // 2
    chunks = 2 if query_cols // head_size % 2 == 0 else 1
    chunk_cols = query_cols // chunks
    weights_first = lax.all_gather(
        jnp.concatenate([query_weight[:, :chunk_cols], keyval_matrix], axis=1),
        "dp", axis=0, tiled=True,
    )
    later_weights = [
        lax.all_gather(query_weight[:, k * chunk_cols:(k + 1) * chunk_cols], "dp", axis=0, tiled=True)
        for k in range(1, chunks)
    ]
    query_first = weights_first[:, :chunk_cols]
    keyval_part = weights_first[:, chunk_cols:]
    all_rows = gather_rows(local_rows, "ctx")
    keyval_cols = keyval_part
    for bit in range(group_bits):
        other = partner(keyval_cols, "ctx", bit)
        upper = device >> bit & 1 == 1
        keyval_cols = jnp.where(
            upper,
            jnp.concatenate([other, keyval_cols], axis=1),
            jnp.concatenate([keyval_cols, other], axis=1),
        )
    projected = jnp.dot(
        all_rows,
        jnp.concatenate([query_first, keyval_cols], axis=1),
        preferred_element_type=jnp.float32,
    ).astype(jnp.bfloat16)
    projected, row_slices = lax.optimization_barrier((projected, row_slices))
    q_chunks = [projected[:, :chunk_cols]]
    keyval_rows = projected[:, chunk_cols:]
    dout_heads = lax.all_to_all(grad_out[0], "ctx", split_axis=1, concat_axis=0, tiled=True)
    group_index = device // group_size
    blk = lax.dynamic_index_in_dim(blocks, group_index, 0, keepdims=False)
    cnt = lax.dynamic_index_in_dim(counts, group_index, 0, keepdims=False)
    row_tokens = lax.all_gather(row_slices, "ctx", axis=1, tiled=True)
    outs, partials, grads = [], None, []
    for k in range(chunks):
        cols = slice(k * chunk_cols, (k + 1) * chunk_cols)
        if k:
            q_chunks.append(
                jnp.dot(all_rows, later_weights[k - 1], preferred_element_type=jnp.float32).astype(
                    jnp.bfloat16
                )
            )
        out_part, dquery, part = attention(
            q_chunks[k], keyval_rows, dout_heads[:, cols], blk, cnt
        )
        if k < chunks - 1:
            later_weights[k], dquery = lax.optimization_barrier((later_weights[k], dquery))
        if k == 0:
            row_tokens, dquery = lax.optimization_barrier((row_tokens, dquery))
        else:
            cotangents, dquery = lax.optimization_barrier((cotangents, dquery))
            grads.append(
                jnp.einsum("spr,spk->rk", row_tokens, cotangents, preferred_element_type=jnp.float32)
            )
        outs.append(out_part)
        partials = part if partials is None else (partials[0] + part[0], partials[1] + part[1])
        if k == chunks - 1:
            summed = scatter_slots(partials[0], partials[1], blk, cnt)
            for bit in range(group_bits):
                summed = summed + partner(summed, "ctx", bit)
            width = summed.shape[1] // group_size
            own_grad = lax.dynamic_slice_in_dim(summed, device % group_size * width, width, 1)
            dquery = jnp.concatenate([dquery, own_grad.astype(jnp.bfloat16)], axis=1)
        cotangents = lax.all_gather(dquery, "dp", axis=0, tiled=False)
    grads.append(
        jnp.einsum("spr,spk->rk", row_tokens, cotangents, preferred_element_type=jnp.float32)
    )
    attended = lax.all_to_all(
        jnp.concatenate(outs, axis=1), "ctx", split_axis=0, concat_axis=1, tiled=True
    )
    grads = jnp.concatenate(grads, axis=1)
    grad_query = grads[:, :query_cols]
    grad_keyval = grads[:, query_cols:]
    return (attended[None], grad_query, grad_keyval)


def solution(mesh):
    in_specs = (
        P("dp", "ctx", None),
        P("dp", "ctx"),
        P("dp", "ctx"),
        P("dp", "ctx", None),
        P(),
        P(),
    )
    out_specs = (P("dp", "ctx", None), P("dp", "ctx"), P("dp", "ctx"))
    return jax.shard_map(shards, mesh=mesh, in_specs=in_specs, out_specs=out_specs, check_vma=False)
```

```python
import jax
import jax.numpy as jnp
from jax import lax
from jax.sharding import PartitionSpec as P


def partner(block, axis, distance):
    count = lax.axis_size(axis)
    route = []
    for low in range(count):
        high = low | 1 << distance
        if high != low and high < count:
            route += [(low, high), (high, low)]
    return lax.ppermute(block, axis, route)


def attend_part(query_rows, key_rows, vals, dout, valid, scale):
    scores = (
        jnp.einsum("nqhd,nkcd->nhqkc", query_rows, key_rows, preferred_element_type=jnp.float32)
        * scale
    )
    scores = jnp.where(valid[:, None, None, :, None], scores, -jnp.inf)
    peak = jnp.max(scores, axis=(3, 4), keepdims=True)
    expo = jnp.exp(scores - peak)
    probs = expo / jnp.sum(expo, axis=(3, 4), keepdims=True)
    probs_b = probs.astype(jnp.bfloat16)
    out = jnp.einsum("nhqkc,nkcd->nqhd", probs_b, vals, preferred_element_type=jnp.float32).astype(
        jnp.bfloat16
    )
    delta = jnp.transpose(
        jnp.sum(dout.astype(jnp.float32) * out.astype(jnp.float32), axis=3), (0, 2, 1)
    )
    dprob = jnp.einsum("nqhd,nkcd->nhqkc", dout, vals, preferred_element_type=jnp.float32)
    dscore = (probs * (dprob - delta[:, :, :, None, None]) * scale).astype(jnp.bfloat16)
    dquery = jnp.einsum(
        "nhqkc,nkcd->nqhd", dscore, key_rows, preferred_element_type=jnp.float32
    ).astype(jnp.bfloat16)
    dkeys = jnp.einsum("nhqkc,nqhd->nkcd", dscore, query_rows, preferred_element_type=jnp.float32)
    dvals = jnp.einsum("nhqkc,nqhd->nkcd", probs_b, dout, preferred_element_type=jnp.float32)
    return (out, dquery, dkeys, dvals)


def attention(q_heads, keyval_rows, dout_heads, blk, cnt):
    length = q_heads.shape[0]
    head_size = keyval_rows.shape[1] // 2
    heads = q_heads.shape[1] // head_size
    nblocks, kslots = blk.shape
    block = length // nblocks
    scale = head_size ** (-0.5)
    step = 4
    groups = nblocks // step
    key_rows = keyval_rows[:, :head_size].reshape(nblocks, block, head_size)
    vals = keyval_rows[:, head_size:].reshape(nblocks, block, head_size)
    valid = lax.broadcasted_iota(jnp.int32, (nblocks, kslots), 1) < cnt[:, None]
    query_rows = q_heads.reshape(groups, step, block, heads, head_size)
    dout = dout_heads.reshape(groups, step, block, heads, head_size)

    def one_step(args):
        q_part, d_part, b_part, v_part = args
        return attend_part(q_part, key_rows[b_part], vals[b_part], d_part, v_part, scale)

    out, dquery, dkeys, dvals = lax.map(
        one_step,
        (query_rows, dout, blk.reshape(groups, step, kslots), valid.reshape(groups, step, kslots)),
    )
    return (
        out.reshape(length, heads * head_size),
        dquery.reshape(length, heads * head_size),
        (dkeys, dvals),
    )


def scatter_slots(dkeys, dvals, blk, cnt):
    nblocks, kslots = blk.shape
    block, head_size = dkeys.shape[-2:]
    length = nblocks * block
    valid = lax.broadcasted_iota(jnp.int32, (nblocks, kslots), 1) < cnt[:, None]
    dkeys = dkeys.reshape(nblocks, kslots, block, head_size)
    dvals = dvals.reshape(nblocks, kslots, block, head_size)
    onehot = (
        (blk[None, :, :] == lax.broadcasted_iota(jnp.int32, (nblocks, 1, 1), 0)) & valid[None]
    ).astype(jnp.float32)
    key_grad = jnp.einsum("bnk,nkcd->bcd", onehot, dkeys, precision=lax.Precision.HIGHEST)
    val_grad = jnp.einsum("bnk,nkcd->bcd", onehot, dvals, precision=lax.Precision.HIGHEST)
    keyval_grad = jnp.concatenate(
        [key_grad.reshape(length, head_size), val_grad.reshape(length, head_size)], axis=1
    )
    return keyval_grad


def exchange_gather(block, axis, order):
    count = lax.axis_size(axis)
    held = block[None]
    for bit in order:
        held = jnp.concatenate([held, partner(held, axis, bit)], axis=0)
    wanted = lax.broadcasted_iota(jnp.int32, (count,), 0) ^ lax.axis_index(axis)
    slot = jnp.zeros((count,), jnp.int32)
    for place, bit in enumerate(order):
        slot = slot | ((wanted >> bit) & 1) << place
    return jnp.take(held, slot, axis=0, mode="clip")


def gather_rows(rows, axis):
    bits = lax.axis_size(axis).bit_length() - 1
    upper = list(range(1, bits))
    half = rows.shape[0] // 2
    first = exchange_gather(rows[:half], axis, upper + [0] if bits else [])
    second = exchange_gather(rows[half:], axis, upper[::-1] + [0] if bits else [])
    return jnp.concatenate([first, second], axis=1).reshape((-1,) + rows.shape[1:])


def shards(tokens, query_weight, keyval_matrix, grad_out, blocks, counts):
    local_rows = tokens[0]
    dp_size = lax.axis_size("dp")
    row_block = local_rows.shape[1] // dp_size
    row_slices = lax.all_to_all(
        local_rows.reshape(local_rows.shape[0], dp_size, row_block).transpose(1, 0, 2),
        "dp", split_axis=0, concat_axis=0, tiled=True,
    )
    group_size = lax.axis_size("ctx") // blocks.shape[0]
    group_bits = group_size.bit_length() - 1
    device = lax.axis_index("ctx")
    query_cols = query_weight.shape[1]
    head_size = keyval_matrix.shape[1] * group_size // 2
    chunks = 2 if query_cols // head_size % 2 == 0 else 1
    chunk_cols = query_cols // chunks
    weights_first = lax.all_gather(
        jnp.concatenate([query_weight[:, :chunk_cols], keyval_matrix], axis=1),
        "dp", axis=0, tiled=True,
    )
    later_weights = [
        lax.all_gather(query_weight[:, k * chunk_cols:(k + 1) * chunk_cols], "dp", axis=0, tiled=True)
        for k in range(1, chunks)
    ]
    query_first = weights_first[:, :chunk_cols]
    keyval_part = weights_first[:, chunk_cols:]
    all_rows = gather_rows(local_rows, "ctx")
    dout_heads = lax.all_to_all(grad_out[0], "ctx", split_axis=1, concat_axis=0, tiled=True)
    all_rows, row_slices, dout_heads = lax.optimization_barrier((all_rows, row_slices, dout_heads))
    keyval_cols = keyval_part
    for bit in range(group_bits):
        other = partner(keyval_cols, "ctx", bit)
        upper = device >> bit & 1 == 1
        keyval_cols = jnp.where(
            upper,
            jnp.concatenate([other, keyval_cols], axis=1),
            jnp.concatenate([keyval_cols, other], axis=1),
        )
    projected = jnp.dot(
        all_rows,
        jnp.concatenate([query_first, keyval_cols], axis=1),
        preferred_element_type=jnp.float32,
    ).astype(jnp.bfloat16)
    q_chunks = [projected[:, :chunk_cols]]
    keyval_rows = projected[:, chunk_cols:]
    group_index = device // group_size
    blk = lax.dynamic_index_in_dim(blocks, group_index, 0, keepdims=False)
    cnt = lax.dynamic_index_in_dim(counts, group_index, 0, keepdims=False)
    row_tokens = lax.all_gather(row_slices, "ctx", axis=1, tiled=True)
    outs, partials, grads = [], None, []
    for k in range(chunks):
        cols = slice(k * chunk_cols, (k + 1) * chunk_cols)
        if k:
            q_chunks.append(
                jnp.dot(all_rows, later_weights[k - 1], preferred_element_type=jnp.float32).astype(
                    jnp.bfloat16
                )
            )
        out_part, dquery, part = attention(
            q_chunks[k], keyval_rows, dout_heads[:, cols], blk, cnt
        )
        if k < chunks - 1:
            later_weights[k], dquery = lax.optimization_barrier((later_weights[k], dquery))
        if k == 0:
            row_tokens, dquery = lax.optimization_barrier((row_tokens, dquery))
        else:
            cotangents, dquery = lax.optimization_barrier((cotangents, dquery))
            grads.append(
                jnp.einsum("spr,spk->rk", row_tokens, cotangents, preferred_element_type=jnp.float32)
            )
        outs.append(out_part)
        partials = part if partials is None else (partials[0] + part[0], partials[1] + part[1])
        if k == chunks - 1:
            summed = scatter_slots(partials[0], partials[1], blk, cnt)
            for bit in range(group_bits):
                summed = summed + partner(summed, "ctx", bit)
            width = summed.shape[1] // group_size
            own_grad = lax.dynamic_slice_in_dim(summed, device % group_size * width, width, 1)
            dquery = jnp.concatenate([dquery, own_grad.astype(jnp.bfloat16)], axis=1)
        cotangents = lax.all_gather(dquery, "dp", axis=0, tiled=False)
    grads.append(
        jnp.einsum("spr,spk->rk", row_tokens, cotangents, preferred_element_type=jnp.float32)
    )
    attended = lax.all_to_all(
        jnp.concatenate(outs, axis=1), "ctx", split_axis=0, concat_axis=1, tiled=True
    )
    grads = jnp.concatenate(grads, axis=1)
    grad_query = grads[:, :query_cols]
    grad_keyval = grads[:, query_cols:]
    return (attended[None], grad_query, grad_keyval)


def solution(mesh):
    in_specs = (
        P("dp", "ctx", None),
        P("dp", "ctx"),
        P("dp", "ctx"),
        P("dp", "ctx", None),
        P(),
        P(),
    )
    out_specs = (P("dp", "ctx", None), P("dp", "ctx"), P("dp", "ctx"))
    return jax.shard_map(shards, mesh=mesh, in_specs=in_specs, out_specs=out_specs, check_vma=False)
```
